128 devices in a mesh: mp: 2 (over y_hi), gx: 32 (over y_lo, z, x), gy: 2 (over core).
Axes of the slice: x: 4, y: 4 (y_hi: 2, y_lo: 2; y = y_hi * 2 + y_lo), z: 4, core: 2. Of those that a mesh axis runs over, the one named last changes fastest.
Arguments:
- tracers: float32 [16, 60, 512, 512], P(None, None, 'gx', ('mp', 'gy')), may hold values from -6 to 6
- wind_courant: float32 [2, 60, 512, 512], P(None, None, 'gx', ('mp', 'gy')), may hold values from -0.45 to 0.45
- pressure_head: float32 [8, 512, 512], P(None, ('gx', 'gy'), 'mp'), may hold values from -2 to 0.5
- storage: float32 [8, 512, 512], P(None, ('gx', 'gy'), 'mp'), may hold values from 0.05 to 0.5
- soil_type: int32 [512, 512], P(('gx', 'gy'), 'mp'), may hold values from 0 to 11
- land_mask: int32 [512, 512], P(('gx', 'gy'), 'mp'), may hold values 0 or 1
- conductivity_table: float32 [12], replicated, may hold values from 0.3 to 3
- exponent_table: float32 [12], replicated, may hold values from 0.2 to 1
Outputs:
- tracers_out: float32 [16, 60, 512, 512], P(None, None, 'gx', ('mp', 'gy'))
- new_head: float32 [8, 512, 512], P(None, ('gx', 'gy'), 'mp')
The draws below stay inside these ranges and needn't reach their ends.
All inputs are finite; a program needn't handle non-finite values. No bound on the sum of `land_mask` on one device may be relied on, other than what follows from the above.
Results may differ from the reference program's by a relative error of at most 0.00002.
Values sent between devices are 32-bit elements; how exact they have to be, the bound alone decides.
No kernel may reach another device: no remote copies, remote signals or barrier semaphores. Data moves between devices by JAX's collectives and lax.ppermute only.
A program may use at most 256 MiB of HBM per device.

```python
import math
import jax
import jax.numpy as jnp
from jax import lax

LEV = 60
NTR = 16
LAY = 8
NSOIL = 12
STEPS = 2
SWEEPS = 3
NXL = 512
NW = 512


def with_ends(values, rng, least, largest):
    shape = values.shape
    index_at = [jax.random.randint(jax.random.fold_in(rng, axis), (), 0, shape[axis]) for axis in range(len(shape))]
    values = values.at[tuple(index_at)].set(least)
    longest = shape.index(max(shape))
    index_at[longest] = (index_at[longest] + 1) % shape[longest]
    return values.at[tuple(index_at)].set(largest)


def shard_levels(own_key, dims, pieces, least, largest):
    factor_of = 1.0
    for position, shards_of in pieces:
        steps = jax.random.uniform(jax.random.fold_in(jax.random.fold_in(own_key, 6), position), (shards_of,), jnp.float32, least / len(pieces), largest / len(pieces))
        factor_of = factor_of * jnp.repeat(jnp.exp(steps), dims[position] // shards_of).reshape((-1,) + (1,) * (len(dims) - 1 - position))
    return factor_of


def gaussian(rng, shape, width, bound, pieces=(), kind=jnp.bfloat16):
    result = jax.random.normal(rng, shape, jnp.float32) * width
    if len(pieces) > 0:
        result = shard_levels(rng, shape, pieces, -0.22, 0.18) * result
    return jnp.clip(result, min=-bound, max=bound).astype(kind)


def setup_inputs(seed: int = 0) -> dict:
    streams_of = jax.random.split(jax.random.key(seed), 9)
    tracers = gaussian(streams_of[0], (NTR, LEV, NXL, NW), 1.0, 6.0, ((2, 32), (3, 4)), jnp.float32)
    wind_courant = jnp.clip(jax.random.uniform(streams_of[1], (2, LEV, NXL, NW), jnp.float32, -0.45, 0.45) * shard_levels(streams_of[1], (2, LEV, NXL, NW), ((2, 32), (3, 4)), -0.4, 0.0), -0.45, 0.45)
    pressure_head = jnp.clip(-2.0 + 2.5 * jax.random.uniform(streams_of[2], (LAY, NXL, NW), jnp.float32) ** shard_levels(streams_of[2], (LAY, NXL, NW), ((1, 64), (2, 2)), -0.2, 0.2), -2.0, 0.5)
    storage = jnp.clip(jnp.exp(math.log(0.5) - 2.3025851 * jax.random.uniform(streams_of[3], (LAY, NXL, NW), jnp.float32) ** shard_levels(streams_of[3], (LAY, NXL, NW), ((1, 64), (2, 2)), -0.2, 0.2)), 0.05, 0.5)
    soil_type = with_ends(jax.random.randint(streams_of[4], (NXL, NW), 0, NSOIL), jax.random.fold_in(streams_of[4], 1), 0, NSOIL - 1).astype(jnp.int32)
    land_mask = with_ends((jax.random.randint(streams_of[5], (NXL, NW), 0, 4) < 3).astype(jnp.int32), jax.random.fold_in(streams_of[5], 1), 0, 1)
    conductivity_table = jnp.clip(jnp.exp(jax.random.uniform(streams_of[6], (NSOIL,), jnp.float32, math.log(0.3), math.log(3.0))), 0.3, 3.0)
    exponent_table = jnp.clip(jnp.exp(jax.random.uniform(streams_of[7], (NSOIL,), jnp.float32, math.log(0.2), math.log(1.0))), 0.2, 1.0)
    return {"tracers": tracers, "wind_courant": wind_courant, "pressure_head": pressure_head, "storage": storage, "soil_type": soil_type, "land_mask": land_mask, "conductivity_table": conductivity_table, "exponent_table": exponent_table}


def advect(padded, wind_along, wind_across):
    mid_field = padded[..., 1:-1]
    mid_wind = wind_along[..., 1:-1]
    flux_along = jnp.maximum(mid_wind[..., :-1, :], 0.0) * mid_field[..., :-1, :] + jnp.minimum(mid_wind[..., 1:, :], 0.0) * mid_field[..., 1:, :]
    row_field = padded[..., 1:-1, :]
    row_wind = wind_across[..., 1:-1, :]
    flux_across = jnp.maximum(row_wind[..., :-1], 0.0) * row_field[..., :-1] + jnp.minimum(row_wind[..., 1:], 0.0) * row_field[..., 1:]
    center = padded[..., 1:-1, 1:-1]
    return center - (flux_along[..., 1:, :] - flux_along[..., :-1, :]) - (flux_across[..., 1:] - flux_across[..., :-1])


def harmonic(first_cond, second_cond):
    return 2.0 * first_cond * second_cond / (first_cond + second_cond)


def sweep(padded, saturated, exponent, capacity, previous, surface):
    conductance = saturated * jnp.exp(exponent * jnp.minimum(padded, 0.0))
    center = conductance[:, 1:-1, 1:-1]
    iterate = padded[:, 1:-1, 1:-1]
    east_face = harmonic(center, conductance[:, 2:, 1:-1])
    west_face = harmonic(center, conductance[:, :-2, 1:-1])
    north_face = harmonic(center, conductance[:, 1:-1, 2:])
    south_face = harmonic(center, conductance[:, 1:-1, :-2])
    lateral = east_face * padded[:, 2:, 1:-1] + west_face * padded[:, :-2, 1:-1] + north_face * padded[:, 1:-1, 2:] + south_face * padded[:, 1:-1, :-2]
    vertical = harmonic(center[:-1], center[1:])
    blank_layer = jnp.zeros_like(center[:1])
    below_face = jnp.concatenate([vertical, blank_layer], axis=0)
    above_face = jnp.concatenate([blank_layer, vertical], axis=0)
    inflow = jnp.concatenate([surface[None], jnp.zeros_like(center[1:])], axis=0)
    drainage = jnp.concatenate([jnp.zeros_like(center[:-1]), center[-1:]], axis=0)
    denominator = capacity + east_face + west_face + north_face + south_face + above_face + below_face
    numerator = capacity * previous + lateral + above_face * jnp.concatenate([blank_layer, iterate[:-1]], axis=0) + below_face * jnp.concatenate([iterate[1:], blank_layer], axis=0) + above_face - below_face + inflow - drainage
    return numerator / denominator


def lookup(soil_kinds, values_table):
    matches = soil_kinds[None] == jnp.arange(values_table.shape[0], dtype=jnp.int32)[:, None, None]
    return jnp.sum(jnp.where(matches, values_table[:, None, None], jnp.float32(0.0)), axis=0)


def pad_cells(field):
    spec = [(0, 0)] * (field.ndim - 2) + [(1, 1), (1, 1)]
    return jnp.pad(field, spec)


def reference(tracers, wind_courant, pressure_head, storage, soil_type, land_mask, conductivity_table, exponent_table):
    wind_along = pad_cells(wind_courant[0])
    wind_across = pad_cells(wind_courant[1])

    def all_steps(field):
        for repeat in range(STEPS):
            field = advect(pad_cells(field), wind_along, wind_across)
        return field

    tracers_out = lax.map(all_steps, tracers)
    precip = jax.nn.softplus(tracers_out[3, 0])
    evaporation = jax.nn.softplus(-tracers_out[1, 0])
    radiation = jax.nn.sigmoid(tracers_out[0, 0]) * jnp.exp(-jax.nn.softplus(tracers_out[2, 0]))
    surface = land_mask.astype(jnp.float32) * (precip - evaporation * radiation)
    saturated = pad_cells(lookup(soil_type, conductivity_table))
    exponent = pad_cells(lookup(soil_type, exponent_table))
    iterate = pressure_head
    for repeat in range(SWEEPS):
        iterate = sweep(pad_cells(iterate), saturated, exponent, storage, pressure_head, surface)
    return tracers_out, iterate
```

```python
import functools
import jax
import jax.numpy as jnp
from jax import lax
from jax.experimental import pallas as pl
from jax.experimental.pallas import tpu as pltpu
from jax.sharding import PartitionSpec as P

SWEEPS = 3
LB = 4


def shift_pairs(count, step):
    if step > 0:
        return [(i, i + 1) for i in range(count - 1)]
    return [(i + 1, i) for i in range(count - 1)]


def step_kernel(emit, nsp, ui, vi, f_ref, w_ref, ftop_ref, fbot_ref, utop_ref, ubot_ref,
                fleft_ref, fright_ref, vleft_ref, vright_ref, o_ref, *edge_refs):
    rows, cols = f_ref.shape[2], f_ref.shape[3]
    chunk = pl.program_id(0)
    row = lax.broadcasted_iota(jnp.int32, (rows, cols), 0)
    lane = lax.broadcasted_iota(jnp.int32, (rows, cols), 1)
    first_row = row == 0
    last_row = row == rows - 1
    first_lane = lane == 0
    last_lane = lane == cols - 1
    if emit:
        r0_ref, r1_ref, c0_ref, c1_ref = edge_refs

        @pl.when(chunk == 0)
        def _():
            c0_ref[...] = jnp.zeros_like(c0_ref)
            c1_ref[...] = jnp.zeros_like(c1_ref)

    for l in range(f_ref.shape[1]):
        lev = chunk * f_ref.shape[1] + l
        to_first = lax.rem(cols - lev, cols)
        to_last = lax.rem(cols - 1 - lev + cols, cols)
        u = w_ref[0, l]
        v = w_ref[1, l]
        u_prev = jnp.where(first_row, utop_ref[l, pl.ds(ui, 1), :], pltpu.roll(u, 1, 0))
        u_next = jnp.where(last_row, ubot_ref[l, pl.ds(ui, 1), :], pltpu.roll(u, rows - 1, 0))
        v_prev = jnp.where(first_lane, pltpu.roll(vleft_ref[vi], to_first, 1), pltpu.roll(v, 1, 1))
        v_next = jnp.where(last_lane, pltpu.roll(vright_ref[vi], to_last, 1), pltpu.roll(v, cols - 1, 1))
        pu = jnp.maximum(u, 0.0)
        mu = jnp.minimum(u, 0.0)
        pu_prev = jnp.maximum(u_prev, 0.0)
        mu_next = jnp.minimum(u_next, 0.0)
        pv = jnp.maximum(v, 0.0)
        mv = jnp.minimum(v, 0.0)
        pv_prev = jnp.maximum(v_prev, 0.0)
        mv_next = jnp.minimum(v_next, 0.0)
        for sp in range(nsp):
            q = f_ref[sp, l]
            q_prev = jnp.where(first_row, ftop_ref[l, pl.ds(sp, 1), :], pltpu.roll(q, 1, 0))
            q_next = jnp.where(last_row, fbot_ref[l, pl.ds(sp, 1), :], pltpu.roll(q, rows - 1, 0))
            q_w = jnp.where(first_lane, pltpu.roll(fleft_ref[sp], to_first, 1), pltpu.roll(q, 1, 1))
            q_e = jnp.where(last_lane, pltpu.roll(fright_ref[sp], to_last, 1), pltpu.roll(q, cols - 1, 1))
            fxp = pu * q + mu_next * q_next
            fxm = pu_prev * q_prev + mu * q
            fyp = pv * q + mv_next * q_e
            fym = pv_prev * q_w + mv * q
            new = q - (fxp - fxm) - (fyp - fym)
            o_ref[sp, l] = new
            if emit:
                r0_ref[l, pl.ds(sp, 1), :] = new[0:1, :]
                r1_ref[l, pl.ds(sp, 1), :] = new[rows - 1:rows, :]
                at_lev = lane == lev
                c0_ref[sp] = jnp.where(at_lev, pltpu.roll(new, lev, 1), c0_ref[sp])
                c1_ref[sp] = jnp.where(at_lev, pltpu.roll(new, lax.rem(lev + 1, cols), 1), c1_ref[sp])


def advect_step(f, w, ftop, fbot, utop, ubot, fleft, fright, vleft, vright, ui, vi, emit):
    nsp, lev, rows, cols = f.shape
    grid = (lev // LB,)
    main = pl.BlockSpec((nsp, LB, rows, cols), lambda c: (0, c, 0, 0))
    wind = pl.BlockSpec((2, LB, rows, cols), lambda c: (0, c, 0, 0))

    def rowspec(a):
        return pl.BlockSpec((LB,) + a.shape[1:], lambda c: (c, 0, 0))

    def whole(a):
        return pl.BlockSpec(a.shape, lambda c: (0,) * a.ndim)

    in_specs = [main, wind, rowspec(ftop), rowspec(fbot), rowspec(utop), rowspec(ubot),
                whole(fleft), whole(fright), whole(vleft), whole(vright)]
    out_shape = [jax.ShapeDtypeStruct(f.shape, f.dtype)]
    out_specs = [main]
    if emit:
        edge_row = jax.ShapeDtypeStruct((lev, nsp, cols), f.dtype)
        edge_col = jax.ShapeDtypeStruct((nsp, rows, cols), f.dtype)
        out_shape += [edge_row, edge_row, edge_col, edge_col]
        out_specs += [pl.BlockSpec((LB, nsp, cols), lambda c: (c, 0, 0))] * 2
        out_specs += [pl.BlockSpec((nsp, rows, cols), lambda c: (0, 0, 0))] * 2
    nbytes = 4 * (2 * f.size + w.size)
    return pl.pallas_call(
        functools.partial(step_kernel, emit, nsp, ui, vi),
        grid=grid,
        in_specs=in_specs,
        out_specs=out_specs,
        out_shape=out_shape,
        compiler_params=pltpu.CompilerParams(dimension_semantics=("arbitrary",)),
        cost_estimate=pl.CostEstimate(flops=20 * f.size, bytes_accessed=nbytes, transcendentals=0),
    )(f, w, ftop, fbot, utop, ubot, fleft, fright, vleft, vright)


def lanes_of_levels(cols_by_level, width):
    moved = jnp.swapaxes(cols_by_level, -1, -2)
    pad = [(0, 0)] * (moved.ndim - 1) + [(0, width - moved.shape[-1])]
    return jnp.pad(moved, pad)


def exchange_rows(first, last):
    n = lax.axis_size("gx")
    top = lax.ppermute(last, "gx", shift_pairs(n, 1))
    bot = lax.ppermute(first, "gx", shift_pairs(n, -1))
    return top, bot


def exchange_cols(first, last):
    axes = ("mp", "gy")
    n = lax.axis_size(axes)
    left = lax.ppermute(last, axes, shift_pairs(n, 1))
    right = lax.ppermute(first, axes, shift_pairs(n, -1))
    return left, right


def advection(tracers, wind_courant):
    nsp, lev, rows, cols = tracers.shape
    row_first = jnp.concatenate(
        [jnp.swapaxes(tracers[:, :, 0, :], 0, 1), wind_courant[0, :, 0, :][:, None, :]], axis=1)
    row_last = jnp.concatenate(
        [jnp.swapaxes(tracers[:, :, rows - 1, :], 0, 1), wind_courant[0, :, rows - 1, :][:, None, :]], axis=1)
    col_first = lanes_of_levels(
        jnp.concatenate([tracers[:, :, :, 0], wind_courant[1:2, :, :, 0]], axis=0), cols)
    col_last = lanes_of_levels(
        jnp.concatenate([tracers[:, :, :, cols - 1], wind_courant[1:2, :, :, cols - 1]], axis=0), cols)
    top, bot = exchange_rows(row_first, row_last)
    left, right = exchange_cols(col_first, col_last)
    mid, r0, r1, c0, c1 = advect_step(
        tracers, wind_courant, top, bot, top, bot, left, right, left, right, nsp, nsp, True)
    top2, bot2 = exchange_rows(r0, r1)
    left2, right2 = exchange_cols(c0, c1)
    (out,) = advect_step(
        mid, wind_courant, top2, bot2, top, bot, left2, right2, left, right, nsp, nsp, False)
    return out


def padded_2(block, sides, width):
    for axis, dim in sides:
        count = lax.axis_size(axis)
        forward = [(i, i + 1) for i in range(count - 1)]
        backward = [(target, source) for source, target in forward]
        low = lax.ppermute(
            lax.slice_in_dim(block, block.shape[dim] - width, None, axis=dim), axis, forward
        )
        high = lax.ppermute(lax.slice_in_dim(block, 0, width, axis=dim), axis, backward)
        block = jnp.concatenate([low, block, high], axis=dim)
    return block


def harmonic(first_cond, second_cond):
    summed = first_cond + second_cond
    return 2.0 * first_cond * second_cond / jnp.where(summed > 0.0, summed, 1.0)


def sweep(padded, saturated, exponent, capacity, previous, surface, outside):
    conductance = saturated * jnp.exp(exponent * jnp.minimum(padded, 0.0))
    center = conductance[:, 1:-1, 1:-1]
    iterate = padded[:, 1:-1, 1:-1]
    east_face = harmonic(center, conductance[:, 2:, 1:-1])
    west_face = harmonic(center, conductance[:, :-2, 1:-1])
    north_face = harmonic(center, conductance[:, 1:-1, 2:])
    south_face = harmonic(center, conductance[:, 1:-1, :-2])
    lateral = (
        east_face * padded[:, 2:, 1:-1]
        + west_face * padded[:, :-2, 1:-1]
        + north_face * padded[:, 1:-1, 2:]
        + south_face * padded[:, 1:-1, :-2]
    )
    vertical = harmonic(center[:-1], center[1:])
    blank_layer = jnp.zeros_like(center[:1])
    below_face = jnp.concatenate([vertical, blank_layer], axis=0)
    above_face = jnp.concatenate([blank_layer, vertical], axis=0)
    inflow = jnp.concatenate([surface[None], jnp.zeros_like(center[1:])], axis=0)
    drainage = jnp.concatenate([jnp.zeros_like(center[:-1]), center[-1:]], axis=0)
    denominator = (
        capacity
        + east_face
        + west_face
        + north_face
        + south_face
        + above_face
        + below_face
        + outside
    )
    numerator = (
        capacity * previous
        + lateral
        + above_face * jnp.concatenate([blank_layer, iterate[:-1]], axis=0)
        + below_face * jnp.concatenate([iterate[1:], blank_layer], axis=0)
        + above_face
        - below_face
        + inflow
        - drainage
    )
    return numerator / denominator


def lookup(soil_kinds, values_table):
    matches = soil_kinds[None] == jnp.arange(values_table.shape[0], dtype=jnp.int32)[:, None, None]
    return jnp.sum(jnp.where(matches, values_table[:, None, None], jnp.float32(0.0)), axis=0)


def forcing_fields(advected):
    precip = jax.nn.softplus(advected[3, 0])
    evaporation = jax.nn.softplus(-advected[1, 0])
    radiation = jax.nn.sigmoid(advected[0, 0]) * jnp.exp(-jax.nn.softplus(advected[2, 0]))
    return jnp.stack([precip, evaporation, radiation], axis=0)


def on_device(
    tracers,
    wind_courant,
    pressure_head,
    storage,
    soil_type,
    land_mask,
    conductivity_table,
    exponent_table,
):
    advected = advection(tracers, wind_courant)
    received = lax.all_to_all(
        forcing_fields(advected), "gy", split_axis=1, concat_axis=2, tiled=True
    )
    surface = land_mask.astype(jnp.float32) * (received[0] - received[1] * received[2])
    saturated = lookup(soil_type, conductivity_table)
    exponent = lookup(soil_type, exponent_table)
    layers = pressure_head.shape[0]
    padded_head = padded_2(
        jnp.concatenate([pressure_head, saturated[None], exponent[None]], axis=0),
        ((("gx", "gy"), 1), ("mp", 2)),
        1,
    )
    saturated_padded = padded_head[layers]
    exponent_padded = padded_head[layers + 1]
    iterate = sweep(
        padded_head[:layers],
        saturated_padded,
        exponent_padded,
        storage,
        pressure_head,
        surface,
        0.0,
    )
    for repeat in range(SWEEPS - 1):
        padded_next = padded_2(iterate, ((("gx", "gy"), 1), ("mp", 2)), 1)
        iterate = sweep(
            padded_next, saturated_padded, exponent_padded, storage, pressure_head, surface, 0.0
        )
    return (advected, iterate)


def solution(mesh):
    placed = (
        P(None, None, "gx", ("mp", "gy")),
        P(None, None, "gx", ("mp", "gy")),
        P(None, ("gx", "gy"), "mp"),
        P(None, ("gx", "gy"), "mp"),
        P(("gx", "gy"), "mp"),
        P(("gx", "gy"), "mp"),
        P(),
        P(),
    )
    return jax.shard_map(
        on_device,
        mesh=mesh,
        in_specs=placed,
        out_specs=(P(None, None, "gx", ("mp", "gy")), P(None, ("gx", "gy"), "mp")),
        check_vma=False,
    )
```

```python
import functools
import jax
import jax.numpy as jnp
from jax import lax
from jax.experimental import pallas as pl
from jax.experimental.pallas import tpu as pltpu
from jax.sharding import PartitionSpec as P

SWEEPS = 3
SB = 2
EB = 4


def shift_pairs(count, step):
    if step > 0:
        return [(i, i + 1) for i in range(count - 1)]
    return [(i + 1, i) for i in range(count - 1)]


def edge_kernel(f_ref, rf_ref, rl_ref, cf_ref, cl_ref):
    nb, nlev, rows, cols = f_ref.shape
    lane = lax.broadcasted_iota(jnp.int32, (rows, cols), 1)
    for b in range(nb):
        acc_f = jnp.zeros((rows, cols), jnp.float32)
        acc_l = jnp.zeros((rows, cols), jnp.float32)
        for lev in range(nlev):
            q = f_ref[b, lev]
            rf_ref[b, pl.ds(lev, 1), :] = q[0:1, :]
            rl_ref[b, pl.ds(lev, 1), :] = q[rows - 1:rows, :]
            at_lev = lane == lev
            acc_f = jnp.where(at_lev, pltpu.roll(q, lev, 1) if lev else q, acc_f)
            acc_l = jnp.where(at_lev, pltpu.roll(q, (lev + 1) % cols, 1), acc_l)
        cf_ref[b] = acc_f
        cl_ref[b] = acc_l


def edges(f):
    n, nlev, rows, cols = f.shape
    nb = EB if n % EB == 0 else 1
    row_shape = jax.ShapeDtypeStruct((n, nlev, cols), f.dtype)
    col_shape = jax.ShapeDtypeStruct((n, rows, cols), f.dtype)
    rspec = pl.BlockSpec((nb, nlev, cols), lambda i: (i, 0, 0))
    cspec = pl.BlockSpec((nb, rows, cols), lambda i: (i, 0, 0))
    return pl.pallas_call(
        edge_kernel,
        grid=(n // nb,),
        in_specs=[pl.BlockSpec((nb, nlev, rows, cols), lambda i: (i, 0, 0, 0))],
        out_specs=[rspec, rspec, cspec, cspec],
        out_shape=[row_shape, row_shape, col_shape, col_shape],
        cost_estimate=pl.CostEstimate(flops=4 * f.size, bytes_accessed=4 * f.size, transcendentals=0),
    )(f)


def step_kernel(f_ref, w_ref, ftop_ref, fbot_ref, wtop_ref, wbot_ref,
                fleft_ref, fright_ref, wleft_ref, wright_ref, o_ref):
    nb, nlev, rows, cols = f_ref.shape
    row = lax.broadcasted_iota(jnp.int32, (rows, cols), 0)
    lane = lax.broadcasted_iota(jnp.int32, (rows, cols), 1)
    first_row = row == 0
    last_row = row == rows - 1
    first_lane = lane == 0
    last_lane = lane == cols - 1

    def to_first(x, lev):
        return pltpu.roll(x, (cols - lev) % cols, 1) if lev else x

    def to_last(x, lev):
        s = (cols - 1 - lev) % cols
        return pltpu.roll(x, s, 1) if s else x

    for lev in range(nlev):
        u = w_ref[0, lev]
        v = w_ref[1, lev]
        u_prev = jnp.where(first_row, wtop_ref[0, pl.ds(lev, 1), :], pltpu.roll(u, 1, 0))
        u_next = jnp.where(last_row, wbot_ref[0, pl.ds(lev, 1), :], pltpu.roll(u, rows - 1, 0))
        v_prev = jnp.where(first_lane, to_first(wleft_ref[1], lev), pltpu.roll(v, 1, 1))
        v_next = jnp.where(last_lane, to_last(wright_ref[1], lev), pltpu.roll(v, cols - 1, 1))
        pu = jnp.maximum(u, 0.0)
        mu = jnp.minimum(u, 0.0)
        pu_prev = jnp.maximum(u_prev, 0.0)
        mu_next = jnp.minimum(u_next, 0.0)
        pv = jnp.maximum(v, 0.0)
        mv = jnp.minimum(v, 0.0)
        pv_prev = jnp.maximum(v_prev, 0.0)
        mv_next = jnp.minimum(v_next, 0.0)
        for b in range(nb):
            q = f_ref[b, lev]
            q_prev = jnp.where(first_row, ftop_ref[b, pl.ds(lev, 1), :], pltpu.roll(q, 1, 0))
            q_next = jnp.where(last_row, fbot_ref[b, pl.ds(lev, 1), :], pltpu.roll(q, rows - 1, 0))
            q_w = jnp.where(first_lane, to_first(fleft_ref[b], lev), pltpu.roll(q, 1, 1))
            q_e = jnp.where(last_lane, to_last(fright_ref[b], lev), pltpu.roll(q, cols - 1, 1))
            fxp = pu * q + mu_next * q_next
            fxm = pu_prev * q_prev + mu * q
            fyp = pv * q + mv_next * q_e
            fym = pv_prev * q_w + mv * q
            o_ref[b, lev] = q - (fxp - fxm) - (fyp - fym)


def advect_step(f, w, ftop, fbot, wtop, wbot, fleft, fright, wleft, wright):
    nsp, nlev, rows, cols = f.shape
    main = pl.BlockSpec((SB, nlev, rows, cols), lambda i: (i, 0, 0, 0))
    rowspec = pl.BlockSpec((SB, nlev, cols), lambda i: (i, 0, 0))
    colspec = pl.BlockSpec((SB, rows, cols), lambda i: (i, 0, 0))

    def whole(a):
        return pl.BlockSpec(a.shape, lambda i: (0,) * a.ndim)

    nbytes = 4 * (2 * f.size + w.size)
    return pl.pallas_call(
        step_kernel,
        grid=(nsp // SB,),
        in_specs=[main, whole(w), rowspec, rowspec, whole(wtop), whole(wbot),
                  colspec, colspec, whole(wleft), whole(wright)],
        out_specs=main,
        out_shape=jax.ShapeDtypeStruct(f.shape, f.dtype),
        cost_estimate=pl.CostEstimate(flops=20 * f.size, bytes_accessed=nbytes, transcendentals=0),
    )(f, w, ftop, fbot, wtop, wbot, fleft, fright, wleft, wright)


def exchange(first, last, axes):
    n = lax.axis_size(axes)
    before = lax.ppermute(last, axes, shift_pairs(n, 1))
    after = lax.ppermute(first, axes, shift_pairs(n, -1))
    return before, after


def advection(tracers, wind_courant):
    cols_axes = ("mp", "gy")
    qrf, qrl, qcf, qcl = edges(tracers)
    wrf, wrl, wcf, wcl = edges(wind_courant)
    qtop, qbot = exchange(qrf, qrl, "gx")
    wtop, wbot = exchange(wrf, wrl, "gx")
    qleft, qright = exchange(qcf, qcl, cols_axes)
    wleft, wright = exchange(wcf, wcl, cols_axes)
    mid = advect_step(tracers, wind_courant, qtop, qbot, wtop, wbot, qleft, qright, wleft, wright)
    srf, srl, scf, scl = edges(mid)
    stop, sbot = exchange(srf, srl, "gx")
    sleft, sright = exchange(scf, scl, cols_axes)
    return advect_step(mid, wind_courant, stop, sbot, wtop, wbot, sleft, sright, wleft, wright)


def padded_2(block, sides, width):
    for axis, dim in sides:
        count = lax.axis_size(axis)
        forward = [(i, i + 1) for i in range(count - 1)]
        backward = [(target, source) for source, target in forward]
        low = lax.ppermute(
            lax.slice_in_dim(block, block.shape[dim] - width, None, axis=dim), axis, forward
        )
        high = lax.ppermute(lax.slice_in_dim(block, 0, width, axis=dim), axis, backward)
        block = jnp.concatenate([low, block, high], axis=dim)
    return block


def harmonic(first_cond, second_cond):
    summed = first_cond + second_cond
    return 2.0 * first_cond * second_cond / jnp.where(summed > 0.0, summed, 1.0)


def sweep(padded, saturated, exponent, capacity, previous, surface, outside):
    conductance = saturated * jnp.exp(exponent * jnp.minimum(padded, 0.0))
    center = conductance[:, 1:-1, 1:-1]
    iterate = padded[:, 1:-1, 1:-1]
    east_face = harmonic(center, conductance[:, 2:, 1:-1])
    west_face = harmonic(center, conductance[:, :-2, 1:-1])
    north_face = harmonic(center, conductance[:, 1:-1, 2:])
    south_face = harmonic(center, conductance[:, 1:-1, :-2])
    lateral = (
        east_face * padded[:, 2:, 1:-1]
        + west_face * padded[:, :-2, 1:-1]
        + north_face * padded[:, 1:-1, 2:]
        + south_face * padded[:, 1:-1, :-2]
    )
    vertical = harmonic(center[:-1], center[1:])
    blank_layer = jnp.zeros_like(center[:1])
    below_face = jnp.concatenate([vertical, blank_layer], axis=0)
    above_face = jnp.concatenate([blank_layer, vertical], axis=0)
    inflow = jnp.concatenate([surface[None], jnp.zeros_like(center[1:])], axis=0)
    drainage = jnp.concatenate([jnp.zeros_like(center[:-1]), center[-1:]], axis=0)
    denominator = (
        capacity
        + east_face
        + west_face
        + north_face
        + south_face
        + above_face
        + below_face
        + outside
    )
    numerator = (
        capacity * previous
        + lateral
        + above_face * jnp.concatenate([blank_layer, iterate[:-1]], axis=0)
        + below_face * jnp.concatenate([iterate[1:], blank_layer], axis=0)
        + above_face
        - below_face
        + inflow
        - drainage
    )
    return numerator / denominator


def lookup(soil_kinds, values_table):
    matches = soil_kinds[None] == jnp.arange(values_table.shape[0], dtype=jnp.int32)[:, None, None]
    return jnp.sum(jnp.where(matches, values_table[:, None, None], jnp.float32(0.0)), axis=0)


def forcing_fields(advected):
    precip = jax.nn.softplus(advected[3, 0])
    evaporation = jax.nn.softplus(-advected[1, 0])
    radiation = jax.nn.sigmoid(advected[0, 0]) * jnp.exp(-jax.nn.softplus(advected[2, 0]))
    return jnp.stack([precip, evaporation, radiation], axis=0)


def on_device(
    tracers,
    wind_courant,
    pressure_head,
    storage,
    soil_type,
    land_mask,
    conductivity_table,
    exponent_table,
):
    advected = advection(tracers, wind_courant)
    received = lax.all_to_all(
        forcing_fields(advected), "gy", split_axis=1, concat_axis=2, tiled=True
    )
    surface = land_mask.astype(jnp.float32) * (received[0] - received[1] * received[2])
    saturated = lookup(soil_type, conductivity_table)
    exponent = lookup(soil_type, exponent_table)
    layers = pressure_head.shape[0]
    padded_head = padded_2(
        jnp.concatenate([pressure_head, saturated[None], exponent[None]], axis=0),
        ((("gx", "gy"), 1), ("mp", 2)),
        1,
    )
    saturated_padded = padded_head[layers]
    exponent_padded = padded_head[layers + 1]
    iterate = sweep(
        padded_head[:layers],
        saturated_padded,
        exponent_padded,
        storage,
        pressure_head,
        surface,
        0.0,
    )
    for repeat in range(SWEEPS - 1):
        padded_next = padded_2(iterate, ((("gx", "gy"), 1), ("mp", 2)), 1)
        iterate = sweep(
            padded_next, saturated_padded, exponent_padded, storage, pressure_head, surface, 0.0
        )
    return (advected, iterate)


def solution(mesh):
    placed = (
        P(None, None, "gx", ("mp", "gy")),
        P(None, None, "gx", ("mp", "gy")),
        P(None, ("gx", "gy"), "mp"),
        P(None, ("gx", "gy"), "mp"),
        P(("gx", "gy"), "mp"),
        P(("gx", "gy"), "mp"),
        P(),
        P(),
    )
    return jax.shard_map(
        on_device,
        mesh=mesh,
        in_specs=placed,
        out_specs=(P(None, None, "gx", ("mp", "gy")), P(None, ("gx", "gy"), "mp")),
        check_vma=False,
    )
```

```python
import functools
import jax
import jax.numpy as jnp
from jax import lax
from jax.experimental import pallas as pl
from jax.experimental.pallas import tpu as pltpu
from jax.sharding import PartitionSpec as P

SWEEPS = 3
SB = 2
EB = 4


def shift_pairs(count, step):
    if step > 0:
        return [(i, i + 1) for i in range(count - 1)]
    return [(i + 1, i) for i in range(count - 1)]


def edge_body(f_ref, b, rf_ref, rl_ref, cf_ref, cl_ref):
    nlev, rows, cols = f_ref.shape[1:]
    lane = lax.broadcasted_iota(jnp.int32, (rows, cols), 1)
    acc_f = jnp.zeros((rows, cols), jnp.float32)
    acc_l = jnp.zeros((rows, cols), jnp.float32)
    for lev in range(nlev):
        q = f_ref[b, lev]
        rf_ref[b, pl.ds(lev, 1), :] = q[0:1, :]
        rl_ref[b, pl.ds(lev, 1), :] = q[rows - 1:rows, :]
        at_lev = lane == lev
        acc_f = jnp.where(at_lev, pltpu.roll(q, lev, 1) if lev else q, acc_f)
        acc_l = jnp.where(at_lev, pltpu.roll(q, (lev + 1) % cols, 1), acc_l)
    cf_ref[b] = acc_f
    cl_ref[b] = acc_l


def edge_kernel(nmain, f_ref, *refs):
    if len(refs) == 5:
        w_ref, outs = refs[0], refs[1:]
    else:
        w_ref, outs = None, refs
    i = pl.program_id(0)

    @pl.when(i < nmain)
    def _():
        for b in range(f_ref.shape[0]):
            edge_body(f_ref, b, *outs)

    if w_ref is not None:
        @pl.when(i == nmain)
        def _():
            for b in range(w_ref.shape[0]):
                edge_body(w_ref, b, *outs)


def edges(f, w=None):
    n, nlev, rows, cols = f.shape
    nb = 2
    nmain = n // nb
    total = n + (0 if w is None else w.shape[0])
    row_shape = jax.ShapeDtypeStruct((total, nlev, cols), f.dtype)
    col_shape = jax.ShapeDtypeStruct((total, rows, cols), f.dtype)
    rspec = pl.BlockSpec((nb, nlev, cols), lambda i: (i, 0, 0))
    cspec = pl.BlockSpec((nb, rows, cols), lambda i: (i, 0, 0))
    in_specs = [pl.BlockSpec((nb, nlev, rows, cols), lambda i: (jnp.minimum(i, nmain - 1), 0, 0, 0))]
    args = [f]
    if w is not None:
        in_specs.append(pl.BlockSpec(w.shape, lambda i: (0, 0, 0, 0)))
        args.append(w)
    return pl.pallas_call(
        functools.partial(edge_kernel, nmain),
        grid=(total // nb,),
        in_specs=in_specs,
        out_specs=[rspec, rspec, cspec, cspec],
        out_shape=[row_shape, row_shape, col_shape, col_shape],
        cost_estimate=pl.CostEstimate(flops=4 * total * nlev * rows * cols,
                                      bytes_accessed=4 * total * nlev * rows * cols, transcendentals=0),
    )(*args)


def step_kernel(f_ref, w_ref, ftop_ref, fbot_ref, wtop_ref, wbot_ref,
                fleft_ref, fright_ref, wleft_ref, wright_ref, o_ref):
    nb, nlev, rows, cols = f_ref.shape
    row = lax.broadcasted_iota(jnp.int32, (rows, cols), 0)
    lane = lax.broadcasted_iota(jnp.int32, (rows, cols), 1)
    first_row = row == 0
    last_row = row == rows - 1
    first_lane = lane == 0
    last_lane = lane == cols - 1

    def to_first(x, lev):
        return pltpu.roll(x, (cols - lev) % cols, 1) if lev else x

    def to_last(x, lev):
        s = (cols - 1 - lev) % cols
        return pltpu.roll(x, s, 1) if s else x

    for lev in range(nlev):
        u = w_ref[0, lev]
        v = w_ref[1, lev]
        u_prev = jnp.where(first_row, wtop_ref[0, pl.ds(lev, 1), :], pltpu.roll(u, 1, 0))
        u_next = jnp.where(last_row, wbot_ref[0, pl.ds(lev, 1), :], pltpu.roll(u, rows - 1, 0))
        v_prev = jnp.where(first_lane, to_first(wleft_ref[1], lev), pltpu.roll(v, 1, 1))
        v_next = jnp.where(last_lane, to_last(wright_ref[1], lev), pltpu.roll(v, cols - 1, 1))
        pu = jnp.maximum(u, 0.0)
        mu = jnp.minimum(u, 0.0)
        pu_prev = jnp.maximum(u_prev, 0.0)
        mu_next = jnp.minimum(u_next, 0.0)
        pv = jnp.maximum(v, 0.0)
        mv = jnp.minimum(v, 0.0)
        pv_prev = jnp.maximum(v_prev, 0.0)
        mv_next = jnp.minimum(v_next, 0.0)
        for b in range(nb):
            q = f_ref[b, lev]
            q_prev = jnp.where(first_row, ftop_ref[b, pl.ds(lev, 1), :], pltpu.roll(q, 1, 0))
            q_next = jnp.where(last_row, fbot_ref[b, pl.ds(lev, 1), :], pltpu.roll(q, rows - 1, 0))
            q_w = jnp.where(first_lane, to_first(fleft_ref[b], lev), pltpu.roll(q, 1, 1))
            q_e = jnp.where(last_lane, to_last(fright_ref[b], lev), pltpu.roll(q, cols - 1, 1))
            fxp = pu * q + mu_next * q_next
            fxm = pu_prev * q_prev + mu * q
            fyp = pv * q + mv_next * q_e
            fym = pv_prev * q_w + mv * q
            o_ref[b, lev] = q - (fxp - fxm) - (fyp - fym)


def advect_step(f, w, ftop, fbot, wtop, wbot, fleft, fright, wleft, wright):
    nsp, nlev, rows, cols = f.shape
    main = pl.BlockSpec((SB, nlev, rows, cols), lambda i: (i, 0, 0, 0))
    rowspec = pl.BlockSpec((SB, nlev, cols), lambda i: (i, 0, 0))
    colspec = pl.BlockSpec((SB, rows, cols), lambda i: (i, 0, 0))
    wblock = nsp // 2
    wrowspec = pl.BlockSpec((2, nlev, cols), lambda i: (wblock, 0, 0))
    wcolspec = pl.BlockSpec((2, rows, cols), lambda i: (wblock, 0, 0))
    nbytes = 4 * (2 * f.size + w.size)
    return pl.pallas_call(
        step_kernel,
        grid=(nsp // SB,),
        in_specs=[main, pl.BlockSpec(w.shape, lambda i: (0, 0, 0, 0)), rowspec, rowspec, wrowspec, wrowspec,
                  colspec, colspec, wcolspec, wcolspec],
        out_specs=main,
        out_shape=jax.ShapeDtypeStruct(f.shape, f.dtype),
        cost_estimate=pl.CostEstimate(flops=20 * f.size, bytes_accessed=nbytes, transcendentals=0),
    )(f, w, ftop, fbot, wtop, wbot, fleft, fright, wleft, wright)


def exchange(first, last, axes):
    n = lax.axis_size(axes)
    before = lax.ppermute(last, axes, shift_pairs(n, 1))
    after = lax.ppermute(first, axes, shift_pairs(n, -1))
    return before, after


def advection(tracers, wind_courant):
    cols_axes = ("mp", "gy")
    rf, rl, cf, cl = edges(tracers, wind_courant)
    top, bot = exchange(rf, rl, "gx")
    left, right = exchange(cf, cl, cols_axes)
    mid = advect_step(tracers, wind_courant, top, bot, top, bot, left, right, left, right)
    srf, srl, scf, scl = edges(mid)
    stop, sbot = exchange(srf, srl, "gx")
    sleft, sright = exchange(scf, scl, cols_axes)
    return advect_step(mid, wind_courant, stop, sbot, top, bot, sleft, sright, left, right)


def padded_2(block, sides, width):
    (row_axes, row_dim), (col_axes, col_dim) = sides
    rows, cols = block.shape[row_dim], block.shape[col_dim]
    top, bot = exchange(lax.slice_in_dim(block, 0, 1, axis=row_dim),
                        lax.slice_in_dim(block, rows - 1, rows, axis=row_dim), row_axes)
    left, right = exchange(lax.slice_in_dim(block, 0, 1, axis=col_dim),
                           lax.slice_in_dim(block, cols - 1, cols, axis=col_dim), col_axes)
    mid = jnp.concatenate([top, block, bot], axis=row_dim)
    spec = [(0, 0)] * block.ndim
    spec[row_dim] = (1, 1)
    left = jnp.pad(left, spec)
    right = jnp.pad(right, spec)
    return jnp.concatenate([left, mid, right], axis=col_dim)


def harmonic(first_cond, second_cond):
    summed = first_cond + second_cond
    return 2.0 * first_cond * second_cond / jnp.where(summed > 0.0, summed, 1.0)


def sweep(padded, saturated, exponent, capacity, previous, surface, outside):
    conductance = saturated * jnp.exp(exponent * jnp.minimum(padded, 0.0))
    center = conductance[:, 1:-1, 1:-1]
    iterate = padded[:, 1:-1, 1:-1]
    east_face = harmonic(center, conductance[:, 2:, 1:-1])
    west_face = harmonic(center, conductance[:, :-2, 1:-1])
    north_face = harmonic(center, conductance[:, 1:-1, 2:])
    south_face = harmonic(center, conductance[:, 1:-1, :-2])
    lateral = (
        east_face * padded[:, 2:, 1:-1]
        + west_face * padded[:, :-2, 1:-1]
        + north_face * padded[:, 1:-1, 2:]
        + south_face * padded[:, 1:-1, :-2]
    )
    vertical = harmonic(center[:-1], center[1:])
    blank_layer = jnp.zeros_like(center[:1])
    below_face = jnp.concatenate([vertical, blank_layer], axis=0)
    above_face = jnp.concatenate([blank_layer, vertical], axis=0)
    inflow = jnp.concatenate([surface[None], jnp.zeros_like(center[1:])], axis=0)
    drainage = jnp.concatenate([jnp.zeros_like(center[:-1]), center[-1:]], axis=0)
    denominator = (
        capacity
        + east_face
        + west_face
        + north_face
        + south_face
        + above_face
        + below_face
        + outside
    )
    numerator = (
        capacity * previous
        + lateral
        + above_face * jnp.concatenate([blank_layer, iterate[:-1]], axis=0)
        + below_face * jnp.concatenate([iterate[1:], blank_layer], axis=0)
        + above_face
        - below_face
        + inflow
        - drainage
    )
    return numerator / denominator


def lookup(soil_kinds, values_table):
    matches = soil_kinds[None] == jnp.arange(values_table.shape[0], dtype=jnp.int32)[:, None, None]
    return jnp.sum(jnp.where(matches, values_table[:, None, None], jnp.float32(0.0)), axis=0)


def forcing_fields(advected):
    precip = jax.nn.softplus(advected[3, 0])
    evaporation = jax.nn.softplus(-advected[1, 0])
    radiation = jax.nn.sigmoid(advected[0, 0]) * jnp.exp(-jax.nn.softplus(advected[2, 0]))
    return jnp.stack([precip, evaporation, radiation], axis=0)


def on_device(
    tracers,
    wind_courant,
    pressure_head,
    storage,
    soil_type,
    land_mask,
    conductivity_table,
    exponent_table,
):
    advected = advection(tracers, wind_courant)
    received = lax.all_to_all(
        forcing_fields(advected), "gy", split_axis=1, concat_axis=2, tiled=True
    )
    surface = land_mask.astype(jnp.float32) * (received[0] - received[1] * received[2])
    saturated = lookup(soil_type, conductivity_table)
    exponent = lookup(soil_type, exponent_table)
    layers = pressure_head.shape[0]
    padded_head = padded_2(
        jnp.concatenate([pressure_head, saturated[None], exponent[None]], axis=0),
        ((("gx", "gy"), 1), ("mp", 2)),
        1,
    )
    saturated_padded = padded_head[layers]
    exponent_padded = padded_head[layers + 1]
    iterate = sweep(
        padded_head[:layers],
        saturated_padded,
        exponent_padded,
        storage,
        pressure_head,
        surface,
        0.0,
    )
    for repeat in range(SWEEPS - 1):
        padded_next = padded_2(iterate, ((("gx", "gy"), 1), ("mp", 2)), 1)
        iterate = sweep(
            padded_next, saturated_padded, exponent_padded, storage, pressure_head, surface, 0.0
        )
    return (advected, iterate)


def solution(mesh):
    placed = (
        P(None, None, "gx", ("mp", "gy")),
        P(None, None, "gx", ("mp", "gy")),
        P(None, ("gx", "gy"), "mp"),
        P(None, ("gx", "gy"), "mp"),
        P(("gx", "gy"), "mp"),
        P(("gx", "gy"), "mp"),
        P(),
        P(),
    )
    return jax.shard_map(
        on_device,
        mesh=mesh,
        in_specs=placed,
        out_specs=(P(None, None, "gx", ("mp", "gy")), P(None, ("gx", "gy"), "mp")),
        check_vma=False,
    )
```

```python
import functools
import jax
import jax.numpy as jnp
from jax import lax
from jax.experimental import pallas as pl
from jax.experimental.pallas import tpu as pltpu
from jax.sharding import PartitionSpec as P

SWEEPS = 3
SB = 2
EB = 4


def shift_pairs(count, step):
    if step > 0:
        return [(i, i + 1) for i in range(count - 1)]
    return [(i + 1, i) for i in range(count - 1)]


def edge_body(f_ref, b, rf_ref, rl_ref, cf_ref, cl_ref):
    nlev, rows, cols = f_ref.shape[1:]
    lane = lax.broadcasted_iota(jnp.int32, (rows, cols), 1)
    acc_f = jnp.zeros((rows, cols), jnp.float32)
    acc_l = jnp.zeros((rows, cols), jnp.float32)
    for lev in range(nlev):
        q = f_ref[b, lev]
        rf_ref[b, pl.ds(lev, 1), :] = q[0:1, :]
        rl_ref[b, pl.ds(lev, 1), :] = q[rows - 1:rows, :]
        at_lev = lane == lev
        acc_f = jnp.where(at_lev, pltpu.roll(q, lev, 1) if lev else q, acc_f)
        acc_l = jnp.where(at_lev, pltpu.roll(q, (lev + 1) % cols, 1), acc_l)
    cf_ref[b] = acc_f
    cl_ref[b] = acc_l


def edge_kernel(nmain, f_ref, *refs):
    if len(refs) == 5:
        w_ref, outs = refs[0], refs[1:]
    else:
        w_ref, outs = None, refs
    i = pl.program_id(0)

    @pl.when(i < nmain)
    def _():
        for b in range(f_ref.shape[0]):
            edge_body(f_ref, b, *outs)

    if w_ref is not None:
        @pl.when(i == nmain)
        def _():
            for b in range(w_ref.shape[0]):
                edge_body(w_ref, b, *outs)


def edges(f, start, count, w=None):
    n, nlev, rows, cols = f.shape
    nb = 2
    nmain = count // nb
    off = start // nb
    total = count + (0 if w is None else w.shape[0])
    row_shape = jax.ShapeDtypeStruct((total, nlev, cols), f.dtype)
    col_shape = jax.ShapeDtypeStruct((total, rows, cols), f.dtype)
    rspec = pl.BlockSpec((nb, nlev, cols), lambda i: (i, 0, 0))
    cspec = pl.BlockSpec((nb, rows, cols), lambda i: (i, 0, 0))
    in_specs = [pl.BlockSpec((nb, nlev, rows, cols), lambda i: (off + jnp.minimum(i, nmain - 1), 0, 0, 0))]
    args = [f]
    if w is not None:
        in_specs.append(pl.BlockSpec(w.shape, lambda i: (0, 0, 0, 0)))
        args.append(w)
    return pl.pallas_call(
        functools.partial(edge_kernel, nmain),
        grid=(total // nb,),
        in_specs=in_specs,
        out_specs=[rspec, rspec, cspec, cspec],
        out_shape=[row_shape, row_shape, col_shape, col_shape],
        cost_estimate=pl.CostEstimate(flops=4 * total * nlev * rows * cols,
                                      bytes_accessed=4 * total * nlev * rows * cols, transcendentals=0),
    )(*args)


def step_kernel(emit, f_ref, w_ref, ftop_ref, fbot_ref, wtop_ref, wbot_ref,
                fleft_ref, fright_ref, wleft_ref, wright_ref, *refs):
    nb, nlev, rows, cols = f_ref.shape
    if emit:
        o_ref, rf_ref, rl_ref, cf_ref, cl_ref = refs
    else:
        o_ref = refs[-1]
    row = lax.broadcasted_iota(jnp.int32, (rows, cols), 0)
    lane = lax.broadcasted_iota(jnp.int32, (rows, cols), 1)
    first_row = row == 0
    last_row = row == rows - 1
    first_lane = lane == 0
    last_lane = lane == cols - 1

    def to_first(x, lev):
        return pltpu.roll(x, (cols - lev) % cols, 1) if lev else x

    def to_last(x, lev):
        sh = (cols - 1 - lev) % cols
        return pltpu.roll(x, sh, 1) if sh else x

    acc_f = [jnp.zeros((rows, cols), jnp.float32) for _ in range(nb)]
    acc_l = [jnp.zeros((rows, cols), jnp.float32) for _ in range(nb)]
    for lev in range(nlev):
        u = w_ref[0, lev]
        v = w_ref[1, lev]
        u_prev = jnp.where(first_row, wtop_ref[0, pl.ds(lev, 1), :], pltpu.roll(u, 1, 0))
        u_next = jnp.where(last_row, wbot_ref[0, pl.ds(lev, 1), :], pltpu.roll(u, rows - 1, 0))
        v_prev = jnp.where(first_lane, to_first(wleft_ref[1], lev), pltpu.roll(v, 1, 1))
        v_next = jnp.where(last_lane, to_last(wright_ref[1], lev), pltpu.roll(v, cols - 1, 1))
        pu = jnp.maximum(u, 0.0)
        mu = jnp.minimum(u, 0.0)
        pu_prev = jnp.maximum(u_prev, 0.0)
        mu_next = jnp.minimum(u_next, 0.0)
        pv = jnp.maximum(v, 0.0)
        mv = jnp.minimum(v, 0.0)
        pv_prev = jnp.maximum(v_prev, 0.0)
        mv_next = jnp.minimum(v_next, 0.0)
        at_lev = lane == lev
        for b in range(nb):
            q = f_ref[b, lev]
            q_prev = jnp.where(first_row, ftop_ref[b, pl.ds(lev, 1), :], pltpu.roll(q, 1, 0))
            q_next = jnp.where(last_row, fbot_ref[b, pl.ds(lev, 1), :], pltpu.roll(q, rows - 1, 0))
            q_w = jnp.where(first_lane, to_first(fleft_ref[b], lev), pltpu.roll(q, 1, 1))
            q_e = jnp.where(last_lane, to_last(fright_ref[b], lev), pltpu.roll(q, cols - 1, 1))
            fxp = pu * q + mu_next * q_next
            fxm = pu_prev * q_prev + mu * q
            fyp = pv * q + mv_next * q_e
            fym = pv_prev * q_w + mv * q
            new = q - (fxp - fxm) - (fyp - fym)
            o_ref[b, lev] = new
            if emit:
                rf_ref[b, pl.ds(lev, 1), :] = new[0:1, :]
                rl_ref[b, pl.ds(lev, 1), :] = new[rows - 1:rows, :]
                acc_f[b] = jnp.where(at_lev, pltpu.roll(new, lev, 1) if lev else new, acc_f[b])
                acc_l[b] = jnp.where(at_lev, pltpu.roll(new, (lev + 1) % cols, 1), acc_l[b])
    if emit:
        for b in range(nb):
            cf_ref[b] = acc_f[b]
            cl_ref[b] = acc_l[b]


def advect_step(f, f_off, count, w, ftop, fbot, wtop, wbot, fleft, fright, wleft, wright,
                emit, into=None, o_off=0, out_total=None):
    nsp, nlev, rows, cols = f.shape
    fo = f_off // SB
    oo = o_off // SB
    src = pl.BlockSpec((SB, nlev, rows, cols), lambda i: (fo + i, 0, 0, 0))
    rowspec = pl.BlockSpec((SB, nlev, cols), lambda i: (i, 0, 0))
    colspec = pl.BlockSpec((SB, rows, cols), lambda i: (i, 0, 0))
    wrowspec = pl.BlockSpec((2, nlev, cols), lambda i: (wtop.shape[0] // 2 - 1, 0, 0))
    wcolspec = pl.BlockSpec((2, rows, cols), lambda i: (wleft.shape[0] // 2 - 1, 0, 0))
    in_specs = [src, pl.BlockSpec(w.shape, lambda i: (0, 0, 0, 0)), rowspec, rowspec, wrowspec, wrowspec,
                colspec, colspec, wcolspec, wcolspec]
    args = [f, w, ftop, fbot, wtop, wbot, fleft, fright, wleft, wright]
    aliases = {}
    if emit:
        out_shape = [jax.ShapeDtypeStruct((count, nlev, rows, cols), f.dtype),
                     jax.ShapeDtypeStruct((count, nlev, cols), f.dtype),
                     jax.ShapeDtypeStruct((count, nlev, cols), f.dtype),
                     jax.ShapeDtypeStruct((count, rows, cols), f.dtype),
                     jax.ShapeDtypeStruct((count, rows, cols), f.dtype)]
        out_specs = [pl.BlockSpec((SB, nlev, rows, cols), lambda i: (i, 0, 0, 0)), rowspec, rowspec,
                     colspec, colspec]
    else:
        total = out_total if into is None else into.shape[0]
        out_shape = jax.ShapeDtypeStruct((total, nlev, rows, cols), f.dtype)
        out_specs = pl.BlockSpec((SB, nlev, rows, cols), lambda i: (oo + i, 0, 0, 0))
        if into is not None:
            in_specs.append(pl.BlockSpec(memory_space=pl.ANY))
            args.append(into)
            aliases = {len(args) - 1: 0}
    nbytes = 4 * (2 * count * nlev * rows * cols + w.size)

    def kernel(*refs):
        if into is not None:
            refs = refs[:10] + refs[11:]
        step_kernel(emit, *refs)

    return pl.pallas_call(
        kernel,
        grid=(count // SB,),
        in_specs=in_specs,
        out_specs=out_specs,
        out_shape=out_shape,
        input_output_aliases=aliases,
        cost_estimate=pl.CostEstimate(flops=20 * count * nlev * rows * cols, bytes_accessed=nbytes,
                                      transcendentals=0),
    )(*args)


def exchange(first, last, axes):
    n = lax.axis_size(axes)
    before = lax.ppermute(last, axes, shift_pairs(n, 1))
    after = lax.ppermute(first, axes, shift_pairs(n, -1))
    return before, after


def advection(tracers, wind_courant):
    cols_axes = ("mp", "gy")
    nsp = tracers.shape[0]
    half = nsp // 2
    phase1 = []
    for c in range(2):
        rf, rl, cf, cl = edges(tracers, c * half, half, wind_courant if c == 0 else None)
        top, bot = exchange(rf, rl, "gx")
        left, right = exchange(cf, cl, cols_axes)
        phase1.append((top, bot, left, right))
    wtop, wbot, wleft, wright = phase1[0]
    phase2 = []
    for c in range(2):
        top, bot, left, right = phase1[c]
        mid, rf, rl, cf, cl = advect_step(tracers, c * half, half, wind_courant, top, bot, wtop, wbot,
                                          left, right, wleft, wright, True)
        stop, sbot = exchange(rf, rl, "gx")
        sleft, sright = exchange(cf, cl, cols_axes)
        phase2.append((mid, stop, sbot, sleft, sright))
    out = None
    for c in range(2):
        mid, stop, sbot, sleft, sright = phase2[c]
        out = advect_step(mid, 0, half, wind_courant, stop, sbot, wtop, wbot, sleft, sright, wleft, wright,
                          False, into=out, o_off=c * half, out_total=nsp)
    return out


def padded_2(block, sides, width):
    (row_axes, row_dim), (col_axes, col_dim) = sides
    rows, cols = block.shape[row_dim], block.shape[col_dim]
    top, bot = exchange(lax.slice_in_dim(block, 0, 1, axis=row_dim),
                        lax.slice_in_dim(block, rows - 1, rows, axis=row_dim), row_axes)
    left, right = exchange(lax.slice_in_dim(block, 0, 1, axis=col_dim),
                           lax.slice_in_dim(block, cols - 1, cols, axis=col_dim), col_axes)
    mid = jnp.concatenate([top, block, bot], axis=row_dim)
    spec = [(0, 0)] * block.ndim
    spec[row_dim] = (1, 1)
    left = jnp.pad(left, spec)
    right = jnp.pad(right, spec)
    return jnp.concatenate([left, mid, right], axis=col_dim)


def harmonic(first_cond, second_cond):
    summed = first_cond + second_cond
    return 2.0 * first_cond * second_cond / jnp.where(summed > 0.0, summed, 1.0)


def sweep(padded, saturated, exponent, capacity, previous, surface, outside):
    conductance = saturated * jnp.exp(exponent * jnp.minimum(padded, 0.0))
    center = conductance[:, 1:-1, 1:-1]
    iterate = padded[:, 1:-1, 1:-1]
    east_face = harmonic(center, conductance[:, 2:, 1:-1])
    west_face = harmonic(center, conductance[:, :-2, 1:-1])
    north_face = harmonic(center, conductance[:, 1:-1, 2:])
    south_face = harmonic(center, conductance[:, 1:-1, :-2])
    lateral = (
        east_face * padded[:, 2:, 1:-1]
        + west_face * padded[:, :-2, 1:-1]
        + north_face * padded[:, 1:-1, 2:]
        + south_face * padded[:, 1:-1, :-2]
    )
    vertical = harmonic(center[:-1], center[1:])
    blank_layer = jnp.zeros_like(center[:1])
    below_face = jnp.concatenate([vertical, blank_layer], axis=0)
    above_face = jnp.concatenate([blank_layer, vertical], axis=0)
    inflow = jnp.concatenate([surface[None], jnp.zeros_like(center[1:])], axis=0)
    drainage = jnp.concatenate([jnp.zeros_like(center[:-1]), center[-1:]], axis=0)
    denominator = (
        capacity
        + east_face
        + west_face
        + north_face
        + south_face
        + above_face
        + below_face
        + outside
    )
    numerator = (
        capacity * previous
        + lateral
        + above_face * jnp.concatenate([blank_layer, iterate[:-1]], axis=0)
        + below_face * jnp.concatenate([iterate[1:], blank_layer], axis=0)
        + above_face
        - below_face
        + inflow
        - drainage
    )
    return numerator / denominator


def lookup(soil_kinds, values_table):
    matches = soil_kinds[None] == jnp.arange(values_table.shape[0], dtype=jnp.int32)[:, None, None]
    return jnp.sum(jnp.where(matches, values_table[:, None, None], jnp.float32(0.0)), axis=0)


def forcing_fields(advected):
    precip = jax.nn.softplus(advected[3, 0])
    evaporation = jax.nn.softplus(-advected[1, 0])
    radiation = jax.nn.sigmoid(advected[0, 0]) * jnp.exp(-jax.nn.softplus(advected[2, 0]))
    return jnp.stack([precip, evaporation, radiation], axis=0)


def on_device(
    tracers,
    wind_courant,
    pressure_head,
    storage,
    soil_type,
    land_mask,
    conductivity_table,
    exponent_table,
):
    advected = advection(tracers, wind_courant)
    received = lax.all_to_all(
        forcing_fields(advected), "gy", split_axis=1, concat_axis=2, tiled=True
    )
    surface = land_mask.astype(jnp.float32) * (received[0] - received[1] * received[2])
    saturated = lookup(soil_type, conductivity_table)
    exponent = lookup(soil_type, exponent_table)
    layers = pressure_head.shape[0]
    padded_head = padded_2(
        jnp.concatenate([pressure_head, saturated[None], exponent[None]], axis=0),
        ((("gx", "gy"), 1), ("mp", 2)),
        1,
    )
    saturated_padded = padded_head[layers]
    exponent_padded = padded_head[layers + 1]
    iterate = sweep(
        padded_head[:layers],
        saturated_padded,
        exponent_padded,
        storage,
        pressure_head,
        surface,
        0.0,
    )
    for repeat in range(SWEEPS - 1):
        padded_next = padded_2(iterate, ((("gx", "gy"), 1), ("mp", 2)), 1)
        iterate = sweep(
            padded_next, saturated_padded, exponent_padded, storage, pressure_head, surface, 0.0
        )
    return (advected, iterate)


def solution(mesh):
    placed = (
        P(None, None, "gx", ("mp", "gy")),
        P(None, None, "gx", ("mp", "gy")),
        P(None, ("gx", "gy"), "mp"),
        P(None, ("gx", "gy"), "mp"),
        P(("gx", "gy"), "mp"),
        P(("gx", "gy"), "mp"),
        P(),
        P(),
    )
    return jax.shard_map(
        on_device,
        mesh=mesh,
        in_specs=placed,
        out_specs=(P(None, None, "gx", ("mp", "gy")), P(None, ("gx", "gy"), "mp")),
        check_vma=False,
    )
```

```python
import functools
import jax
import jax.numpy as jnp
from jax import lax
from jax.experimental import pallas as pl
from jax.experimental.pallas import tpu as pltpu
from jax.sharding import PartitionSpec as P

SWEEPS = 3
SB = 2
EB = 4


def shift_pairs(count, step):
    if step > 0:
        return [(i, i + 1) for i in range(count - 1)]
    return [(i + 1, i) for i in range(count - 1)]


def edge_body(f_ref, b, rf_ref, rl_ref, cf_ref, cl_ref):
    nlev, rows, cols = f_ref.shape[1:]
    lane = lax.broadcasted_iota(jnp.int32, (rows, cols), 1)
    acc_f = jnp.zeros((rows, cols), jnp.float32)
    acc_l = jnp.zeros((rows, cols), jnp.float32)
    for lev in range(nlev):
        q = f_ref[b, lev]
        rf_ref[b, pl.ds(lev, 1), :] = q[0:1, :]
        rl_ref[b, pl.ds(lev, 1), :] = q[rows - 1:rows, :]
        at_lev = lane == lev
        acc_f = jnp.where(at_lev, pltpu.roll(q, lev, 1) if lev else q, acc_f)
        acc_l = jnp.where(at_lev, pltpu.roll(q, (lev + 1) % cols, 1), acc_l)
    cf_ref[b] = acc_f
    cl_ref[b] = acc_l


def edge_kernel(nmain, f_ref, *refs):
    if len(refs) == 5:
        w_ref, outs = refs[0], refs[1:]
    else:
        w_ref, outs = None, refs
    i = pl.program_id(0)

    @pl.when(i < nmain)
    def _():
        for b in range(f_ref.shape[0]):
            edge_body(f_ref, b, *outs)

    if w_ref is not None:
        @pl.when(i == nmain)
        def _():
            for b in range(w_ref.shape[0]):
                edge_body(w_ref, b, *outs)


def edges(f, w=None):
    n, nlev, rows, cols = f.shape
    nb = 2
    nmain = n // nb
    total = n + (0 if w is None else w.shape[0])
    row_shape = jax.ShapeDtypeStruct((total, nlev, cols), f.dtype)
    col_shape = jax.ShapeDtypeStruct((total, rows, cols), f.dtype)
    rspec = pl.BlockSpec((nb, nlev, cols), lambda i: (i, 0, 0))
    cspec = pl.BlockSpec((nb, rows, cols), lambda i: (i, 0, 0))
    in_specs = [pl.BlockSpec((nb, nlev, rows, cols), lambda i: (jnp.minimum(i, nmain - 1), 0, 0, 0))]
    args = [f]
    if w is not None:
        in_specs.append(pl.BlockSpec(w.shape, lambda i: (0, 0, 0, 0)))
        args.append(w)
    return pl.pallas_call(
        functools.partial(edge_kernel, nmain),
        grid=(total // nb,),
        in_specs=in_specs,
        out_specs=[rspec, rspec, cspec, cspec],
        out_shape=[row_shape, row_shape, col_shape, col_shape],
        cost_estimate=pl.CostEstimate(flops=4 * total * nlev * rows * cols,
                                      bytes_accessed=4 * total * nlev * rows * cols, transcendentals=0),
    )(*args)


def step_kernel(f_ref, w_ref, ftop_ref, fbot_ref, wtop_ref, wbot_ref,
                fleft_ref, fright_ref, wleft_ref, wright_ref, o_ref):
    nb, nlev, rows, cols = f_ref.shape
    row = lax.broadcasted_iota(jnp.int32, (rows, cols), 0)
    lane = lax.broadcasted_iota(jnp.int32, (rows, cols), 1)
    first_row = row == 0
    last_row = row == rows - 1
    first_lane = lane == 0
    last_lane = lane == cols - 1

    def to_first(x, lev):
        return pltpu.roll(x, (cols - lev) % cols, 1) if lev else x

    def to_last(x, lev):
        s = (cols - 1 - lev) % cols
        return pltpu.roll(x, s, 1) if s else x

    for lev in range(nlev):
        u = w_ref[0, lev]
        v = w_ref[1, lev]
        u_prev = jnp.where(first_row, wtop_ref[0, pl.ds(lev, 1), :], pltpu.roll(u, 1, 0))
        u_next = jnp.where(last_row, wbot_ref[0, pl.ds(lev, 1), :], pltpu.roll(u, rows - 1, 0))
        v_prev = jnp.where(first_lane, to_first(wleft_ref[1], lev), pltpu.roll(v, 1, 1))
        v_next = jnp.where(last_lane, to_last(wright_ref[1], lev), pltpu.roll(v, cols - 1, 1))
        pu = jnp.maximum(u, 0.0)
        mu = jnp.minimum(u, 0.0)
        pu_prev = jnp.maximum(u_prev, 0.0)
        mu_next = jnp.minimum(u_next, 0.0)
        pv = jnp.maximum(v, 0.0)
        mv = jnp.minimum(v, 0.0)
        pv_prev = jnp.maximum(v_prev, 0.0)
        mv_next = jnp.minimum(v_next, 0.0)
        for b in range(nb):
            q = f_ref[b, lev]
            q_prev = jnp.where(first_row, ftop_ref[b, pl.ds(lev, 1), :], pltpu.roll(q, 1, 0))
            q_next = jnp.where(last_row, fbot_ref[b, pl.ds(lev, 1), :], pltpu.roll(q, rows - 1, 0))
            q_w = jnp.where(first_lane, to_first(fleft_ref[b], lev), pltpu.roll(q, 1, 1))
            q_e = jnp.where(last_lane, to_last(fright_ref[b], lev), pltpu.roll(q, cols - 1, 1))
            fxp = pu * q + mu_next * q_next
            fxm = pu_prev * q_prev + mu * q
            fyp = pv * q + mv_next * q_e
            fym = pv_prev * q_w + mv * q
            o_ref[b, lev] = q - (fxp - fxm) - (fyp - fym)


def advect_step(f, w, ftop, fbot, wtop, wbot, fleft, fright, wleft, wright):
    nsp, nlev, rows, cols = f.shape
    main = pl.BlockSpec((SB, nlev, rows, cols), lambda i: (i, 0, 0, 0))
    rowspec = pl.BlockSpec((SB, nlev, cols), lambda i: (i, 0, 0))
    colspec = pl.BlockSpec((SB, rows, cols), lambda i: (i, 0, 0))
    wblock = nsp // 2
    wrowspec = pl.BlockSpec((2, nlev, cols), lambda i: (wblock, 0, 0))
    wcolspec = pl.BlockSpec((2, rows, cols), lambda i: (wblock, 0, 0))
    nbytes = 4 * (2 * f.size + w.size)
    return pl.pallas_call(
        step_kernel,
        grid=(nsp // SB,),
        in_specs=[main, pl.BlockSpec(w.shape, lambda i: (0, 0, 0, 0)), rowspec, rowspec, wrowspec, wrowspec,
                  colspec, colspec, wcolspec, wcolspec],
        out_specs=main,
        out_shape=jax.ShapeDtypeStruct(f.shape, f.dtype),
        cost_estimate=pl.CostEstimate(flops=20 * f.size, bytes_accessed=nbytes, transcendentals=0),
    )(f, w, ftop, fbot, wtop, wbot, fleft, fright, wleft, wright)


def exchange(first, last, axes):
    n = lax.axis_size(axes)
    before = lax.ppermute(last, axes, shift_pairs(n, 1))
    after = lax.ppermute(first, axes, shift_pairs(n, -1))
    return before, after


def advection(tracers, wind_courant, soil_block):
    cols_axes = ("mp", "gy")
    rf, rl, cf, cl = edges(tracers, wind_courant)
    top, bot = exchange(rf, rl, "gx")
    left, right = exchange(cf, cl, cols_axes)
    mid = advect_step(tracers, wind_courant, top, bot, top, bot, left, right, left, right)
    mid, soil_block = lax.optimization_barrier((mid, soil_block))
    srf, srl, scf, scl = edges(mid)
    stop, sbot = exchange(srf, srl, "gx")
    sleft, sright = exchange(scf, scl, cols_axes)
    return advect_step(mid, wind_courant, stop, sbot, top, bot, sleft, sright, left, right), soil_block


def padded_2(block, sides, width):
    (row_axes, row_dim), (col_axes, col_dim) = sides
    rows, cols = block.shape[row_dim], block.shape[col_dim]
    top, bot = exchange(lax.slice_in_dim(block, 0, 1, axis=row_dim),
                        lax.slice_in_dim(block, rows - 1, rows, axis=row_dim), row_axes)
    left, right = exchange(lax.slice_in_dim(block, 0, 1, axis=col_dim),
                           lax.slice_in_dim(block, cols - 1, cols, axis=col_dim), col_axes)
    mid = jnp.concatenate([top, block, bot], axis=row_dim)
    spec = [(0, 0)] * block.ndim
    spec[row_dim] = (1, 1)
    left = jnp.pad(left, spec)
    right = jnp.pad(right, spec)
    return jnp.concatenate([left, mid, right], axis=col_dim)


def harmonic(first_cond, second_cond):
    summed = first_cond + second_cond
    return 2.0 * first_cond * second_cond / jnp.where(summed > 0.0, summed, 1.0)


def sweep(padded, saturated, exponent, capacity, previous, surface, outside):
    conductance = saturated * jnp.exp(exponent * jnp.minimum(padded, 0.0))
    center = conductance[:, 1:-1, 1:-1]
    iterate = padded[:, 1:-1, 1:-1]
    east_face = harmonic(center, conductance[:, 2:, 1:-1])
    west_face = harmonic(center, conductance[:, :-2, 1:-1])
    north_face = harmonic(center, conductance[:, 1:-1, 2:])
    south_face = harmonic(center, conductance[:, 1:-1, :-2])
    lateral = (
        east_face * padded[:, 2:, 1:-1]
        + west_face * padded[:, :-2, 1:-1]
        + north_face * padded[:, 1:-1, 2:]
        + south_face * padded[:, 1:-1, :-2]
    )
    vertical = harmonic(center[:-1], center[1:])
    blank_layer = jnp.zeros_like(center[:1])
    below_face = jnp.concatenate([vertical, blank_layer], axis=0)
    above_face = jnp.concatenate([blank_layer, vertical], axis=0)
    inflow = jnp.concatenate([surface[None], jnp.zeros_like(center[1:])], axis=0)
    drainage = jnp.concatenate([jnp.zeros_like(center[:-1]), center[-1:]], axis=0)
    denominator = (
        capacity
        + east_face
        + west_face
        + north_face
        + south_face
        + above_face
        + below_face
        + outside
    )
    numerator = (
        capacity * previous
        + lateral
        + above_face * jnp.concatenate([blank_layer, iterate[:-1]], axis=0)
        + below_face * jnp.concatenate([iterate[1:], blank_layer], axis=0)
        + above_face
        - below_face
        + inflow
        - drainage
    )
    return numerator / denominator


def lookup(soil_kinds, values_table):
    matches = soil_kinds[None] == jnp.arange(values_table.shape[0], dtype=jnp.int32)[:, None, None]
    return jnp.sum(jnp.where(matches, values_table[:, None, None], jnp.float32(0.0)), axis=0)


def forcing_fields(advected):
    precip = jax.nn.softplus(advected[3, 0])
    evaporation = jax.nn.softplus(-advected[1, 0])
    radiation = jax.nn.sigmoid(advected[0, 0]) * jnp.exp(-jax.nn.softplus(advected[2, 0]))
    return jnp.stack([precip, evaporation, radiation], axis=0)


def on_device(
    tracers,
    wind_courant,
    pressure_head,
    storage,
    soil_type,
    land_mask,
    conductivity_table,
    exponent_table,
):
    saturated = lookup(soil_type, conductivity_table)
    exponent = lookup(soil_type, exponent_table)
    soil_block = jnp.concatenate([pressure_head, saturated[None], exponent[None]], axis=0)
    advected, soil_block = advection(tracers, wind_courant, soil_block)
    received = lax.all_to_all(
        forcing_fields(advected), "gy", split_axis=1, concat_axis=2, tiled=True
    )
    surface = land_mask.astype(jnp.float32) * (received[0] - received[1] * received[2])
    saturated = lookup(soil_type, conductivity_table)
    exponent = lookup(soil_type, exponent_table)
    layers = pressure_head.shape[0]
    padded_head = padded_2(
        soil_block,
        ((("gx", "gy"), 1), ("mp", 2)),
        1,
    )
    saturated_padded = padded_head[layers]
    exponent_padded = padded_head[layers + 1]
    iterate = sweep(
        padded_head[:layers],
        saturated_padded,
        exponent_padded,
        storage,
        pressure_head,
        surface,
        0.0,
    )
    for repeat in range(SWEEPS - 1):
        padded_next = padded_2(iterate, ((("gx", "gy"), 1), ("mp", 2)), 1)
        iterate = sweep(
            padded_next, saturated_padded, exponent_padded, storage, pressure_head, surface, 0.0
        )
    return (advected, iterate)


def solution(mesh):
    placed = (
        P(None, None, "gx", ("mp", "gy")),
        P(None, None, "gx", ("mp", "gy")),
        P(None, ("gx", "gy"), "mp"),
        P(None, ("gx", "gy"), "mp"),
        P(("gx", "gy"), "mp"),
        P(("gx", "gy"), "mp"),
        P(),
        P(),
    )
    return jax.shard_map(
        on_device,
        mesh=mesh,
        in_specs=placed,
        out_specs=(P(None, None, "gx", ("mp", "gy")), P(None, ("gx", "gy"), "mp")),
        check_vma=False,
    )
```

```python
import functools
import jax
import jax.numpy as jnp
from jax import lax
from jax.experimental import pallas as pl
from jax.experimental.pallas import tpu as pltpu
from jax.sharding import PartitionSpec as P

SWEEPS = 3
SB = 2
EB = 4


def shift_pairs(count, step):
    if step > 0:
        return [(i, i + 1) for i in range(count - 1)]
    return [(i + 1, i) for i in range(count - 1)]


def edge_body(f_ref, b, rf_ref, rl_ref, cf_ref, cl_ref):
    nlev, rows, cols = f_ref.shape[1:]
    lane = lax.broadcasted_iota(jnp.int32, (rows, cols), 1)
    acc_f = jnp.zeros((rows, cols), jnp.float32)
    acc_l = jnp.zeros((rows, cols), jnp.float32)
    for lev in range(nlev):
        q = f_ref[b, lev]
        rf_ref[b, pl.ds(lev, 1), :] = q[0:1, :]
        rl_ref[b, pl.ds(lev, 1), :] = q[rows - 1:rows, :]
        at_lev = lane == lev
        acc_f = jnp.where(at_lev, pltpu.roll(q, lev, 1) if lev else q, acc_f)
        acc_l = jnp.where(at_lev, pltpu.roll(q, (lev + 1) % cols, 1), acc_l)
    cf_ref[b] = acc_f
    cl_ref[b] = acc_l


def edge_kernel(nmain, f_ref, *refs):
    if len(refs) == 5:
        w_ref, outs = refs[0], refs[1:]
    else:
        w_ref, outs = None, refs
    i = pl.program_id(0)

    @pl.when(i < nmain)
    def _():
        for b in range(f_ref.shape[0]):
            edge_body(f_ref, b, *outs)

    if w_ref is not None:
        @pl.when(i == nmain)
        def _():
            for b in range(w_ref.shape[0]):
                edge_body(w_ref, b, *outs)


def edges(f, w=None):
    n, nlev, rows, cols = f.shape
    nb = 2
    nmain = n // nb
    total = n + (0 if w is None else w.shape[0])
    row_shape = jax.ShapeDtypeStruct((total, nlev, cols), f.dtype)
    col_shape = jax.ShapeDtypeStruct((total, rows, cols), f.dtype)
    rspec = pl.BlockSpec((nb, nlev, cols), lambda i: (i, 0, 0))
    cspec = pl.BlockSpec((nb, rows, cols), lambda i: (i, 0, 0))
    in_specs = [pl.BlockSpec((nb, nlev, rows, cols), lambda i: (jnp.minimum(i, nmain - 1), 0, 0, 0))]
    args = [f]
    if w is not None:
        in_specs.append(pl.BlockSpec(w.shape, lambda i: (0, 0, 0, 0)))
        args.append(w)
    return pl.pallas_call(
        functools.partial(edge_kernel, nmain),
        grid=(total // nb,),
        in_specs=in_specs,
        out_specs=[rspec, rspec, cspec, cspec],
        out_shape=[row_shape, row_shape, col_shape, col_shape],
        cost_estimate=pl.CostEstimate(flops=4 * total * nlev * rows * cols,
                                      bytes_accessed=4 * total * nlev * rows * cols, transcendentals=0),
    )(*args)


def step_kernel(f_ref, w_ref, ftop_ref, fbot_ref, wtop_ref, wbot_ref,
                fleft_ref, fright_ref, wleft_ref, wright_ref, o_ref):
    nb, nlev, rows, cols = f_ref.shape
    row = lax.broadcasted_iota(jnp.int32, (rows, cols), 0)
    lane = lax.broadcasted_iota(jnp.int32, (rows, cols), 1)
    first_row = row == 0
    last_row = row == rows - 1
    first_lane = lane == 0
    last_lane = lane == cols - 1

    def to_first(x, lev):
        return pltpu.roll(x, (cols - lev) % cols, 1) if lev else x

    def to_last(x, lev):
        s = (cols - 1 - lev) % cols
        return pltpu.roll(x, s, 1) if s else x

    for lev in range(nlev):
        u = w_ref[0, lev]
        v = w_ref[1, lev]
        u_prev = jnp.where(first_row, wtop_ref[0, pl.ds(lev, 1), :], pltpu.roll(u, 1, 0))
        u_next = jnp.where(last_row, wbot_ref[0, pl.ds(lev, 1), :], pltpu.roll(u, rows - 1, 0))
        v_prev = jnp.where(first_lane, to_first(wleft_ref[1], lev), pltpu.roll(v, 1, 1))
        v_next = jnp.where(last_lane, to_last(wright_ref[1], lev), pltpu.roll(v, cols - 1, 1))
        pu = jnp.maximum(u, 0.0)
        mu = jnp.minimum(u, 0.0)
        pu_prev = jnp.maximum(u_prev, 0.0)
        mu_next = jnp.minimum(u_next, 0.0)
        pv = jnp.maximum(v, 0.0)
        mv = jnp.minimum(v, 0.0)
        pv_prev = jnp.maximum(v_prev, 0.0)
        mv_next = jnp.minimum(v_next, 0.0)
        for b in range(nb):
            q = f_ref[b, lev]
            q_prev = jnp.where(first_row, ftop_ref[b, pl.ds(lev, 1), :], pltpu.roll(q, 1, 0))
            q_next = jnp.where(last_row, fbot_ref[b, pl.ds(lev, 1), :], pltpu.roll(q, rows - 1, 0))
            q_w = jnp.where(first_lane, to_first(fleft_ref[b], lev), pltpu.roll(q, 1, 1))
            q_e = jnp.where(last_lane, to_last(fright_ref[b], lev), pltpu.roll(q, cols - 1, 1))
            fxp = pu * q + mu_next * q_next
            fxm = pu_prev * q_prev + mu * q
            fyp = pv * q + mv_next * q_e
            fym = pv_prev * q_w + mv * q
            o_ref[b, lev] = q - (fxp - fxm) - (fyp - fym)


def advect_step(f, w, ftop, fbot, wtop, wbot, fleft, fright, wleft, wright):
    nsp, nlev, rows, cols = f.shape
    main = pl.BlockSpec((SB, nlev, rows, cols), lambda i: (i, 0, 0, 0))
    rowspec = pl.BlockSpec((SB, nlev, cols), lambda i: (i, 0, 0))
    colspec = pl.BlockSpec((SB, rows, cols), lambda i: (i, 0, 0))
    wblock = nsp // 2
    wrowspec = pl.BlockSpec((2, nlev, cols), lambda i: (wblock, 0, 0))
    wcolspec = pl.BlockSpec((2, rows, cols), lambda i: (wblock, 0, 0))
    nbytes = 4 * (2 * f.size + w.size)
    return pl.pallas_call(
        step_kernel,
        grid=(nsp // SB,),
        in_specs=[main, pl.BlockSpec(w.shape, lambda i: (0, 0, 0, 0)), rowspec, rowspec, wrowspec, wrowspec,
                  colspec, colspec, wcolspec, wcolspec],
        out_specs=main,
        out_shape=jax.ShapeDtypeStruct(f.shape, f.dtype),
        cost_estimate=pl.CostEstimate(flops=20 * f.size, bytes_accessed=nbytes, transcendentals=0),
    )(f, w, ftop, fbot, wtop, wbot, fleft, fright, wleft, wright)


def exchange(first, last, axes):
    n = lax.axis_size(axes)
    before = lax.ppermute(last, axes, shift_pairs(n, 1))
    after = lax.ppermute(first, axes, shift_pairs(n, -1))
    return before, after


def open_kernel(f_ref, w_ref, o_ref):
    nb, nlev, rows, cols = f_ref.shape
    row = lax.broadcasted_iota(jnp.int32, (rows, cols), 0)
    lane = lax.broadcasted_iota(jnp.int32, (rows, cols), 1)
    first_row = row == 0
    last_row = row == rows - 1
    first_lane = lane == 0
    last_lane = lane == cols - 1
    for lev in range(nlev):
        u = w_ref[0, lev]
        v = w_ref[1, lev]
        u_prev = jnp.where(first_row, 0.0, pltpu.roll(u, 1, 0))
        u_next = jnp.where(last_row, 0.0, pltpu.roll(u, rows - 1, 0))
        v_prev = jnp.where(first_lane, 0.0, pltpu.roll(v, 1, 1))
        v_next = jnp.where(last_lane, 0.0, pltpu.roll(v, cols - 1, 1))
        pu = jnp.maximum(u, 0.0)
        mu = jnp.minimum(u, 0.0)
        pu_prev = jnp.maximum(u_prev, 0.0)
        mu_next = jnp.minimum(u_next, 0.0)
        pv = jnp.maximum(v, 0.0)
        mv = jnp.minimum(v, 0.0)
        pv_prev = jnp.maximum(v_prev, 0.0)
        mv_next = jnp.minimum(v_next, 0.0)
        for b in range(nb):
            q = f_ref[b, lev]
            q_prev = pltpu.roll(q, 1, 0)
            q_next = pltpu.roll(q, rows - 1, 0)
            q_w = pltpu.roll(q, 1, 1)
            q_e = pltpu.roll(q, cols - 1, 1)
            fxp = pu * q + mu_next * q_next
            fxm = pu_prev * q_prev + mu * q
            fyp = pv * q + mv_next * q_e
            fym = pv_prev * q_w + mv * q
            o_ref[b, lev] = q - (fxp - fxm) - (fyp - fym)


def open_step(f, w):
    nsp, nlev, rows, cols = f.shape
    main = pl.BlockSpec((SB, nlev, rows, cols), lambda i: (i, 0, 0, 0))
    return pl.pallas_call(
        open_kernel,
        grid=(nsp // SB,),
        in_specs=[main, pl.BlockSpec(w.shape, lambda i: (0, 0, 0, 0))],
        out_specs=main,
        out_shape=jax.ShapeDtypeStruct(f.shape, f.dtype),
        cost_estimate=pl.CostEstimate(flops=20 * f.size, bytes_accessed=4 * (2 * f.size + w.size),
                                      transcendentals=0),
    )(f, w)


def fix_kernel(emit, s_ref, ftop_ref, fbot_ref, wtop_ref, wbot_ref, fleft_ref, fright_ref,
               wleft_ref, wright_ref, o_ref, *edge_refs):
    nb, nlev, rows, cols = s_ref.shape
    row = lax.broadcasted_iota(jnp.int32, (rows, cols), 0)
    lane = lax.broadcasted_iota(jnp.int32, (rows, cols), 1)
    first_row = row == 0
    last_row = row == rows - 1
    first_lane = lane == 0
    last_lane = lane == cols - 1

    def to_first(x, lev):
        return pltpu.roll(x, (cols - lev) % cols, 1) if lev else x

    def to_last(x, lev):
        sh = (cols - 1 - lev) % cols
        return pltpu.roll(x, sh, 1) if sh else x

    if emit:
        rf_ref, rl_ref, cf_ref, cl_ref = edge_refs
    wl = wleft_ref[1]
    wr = wright_ref[1]
    for b in range(nb):
        acc_f = jnp.zeros((rows, cols), jnp.float32)
        acc_l = jnp.zeros((rows, cols), jnp.float32)
        fl = fleft_ref[b]
        fr = fright_ref[b]
        for lev in range(nlev):
            x = s_ref[b, lev]
            top = jnp.maximum(wtop_ref[0, pl.ds(lev, 1), :], 0.0) * ftop_ref[b, pl.ds(lev, 1), :]
            bot = jnp.minimum(wbot_ref[0, pl.ds(lev, 1), :], 0.0) * fbot_ref[b, pl.ds(lev, 1), :]
            left = jnp.maximum(to_first(wl, lev), 0.0) * to_first(fl, lev)
            right = jnp.minimum(to_last(wr, lev), 0.0) * to_last(fr, lev)
            x = jnp.where(first_row, x + top, x)
            x = jnp.where(last_row, x - bot, x)
            x = jnp.where(first_lane, x + left, x)
            x = jnp.where(last_lane, x - right, x)
            o_ref[b, lev] = x
            if emit:
                rf_ref[b, pl.ds(lev, 1), :] = x[0:1, :]
                rl_ref[b, pl.ds(lev, 1), :] = x[rows - 1:rows, :]
                at_lev = lane == lev
                acc_f = jnp.where(at_lev, pltpu.roll(x, lev, 1) if lev else x, acc_f)
                acc_l = jnp.where(at_lev, pltpu.roll(x, (lev + 1) % cols, 1), acc_l)
        if emit:
            cf_ref[b] = acc_f
            cl_ref[b] = acc_l


def fix_step(s, ftop, fbot, wtop, wbot, fleft, fright, wleft, wright, emit):
    nsp, nlev, rows, cols = s.shape
    main = pl.BlockSpec((SB, nlev, rows, cols), lambda i: (i, 0, 0, 0))
    rowspec = pl.BlockSpec((SB, nlev, cols), lambda i: (i, 0, 0))
    colspec = pl.BlockSpec((SB, rows, cols), lambda i: (i, 0, 0))
    wrowspec = pl.BlockSpec((2, nlev, cols), lambda i: (wtop.shape[0] // 2 - 1, 0, 0))
    wcolspec = pl.BlockSpec((2, rows, cols), lambda i: (wleft.shape[0] // 2 - 1, 0, 0))
    out_shape = [jax.ShapeDtypeStruct(s.shape, s.dtype)]
    out_specs = [main]
    if emit:
        out_shape += [jax.ShapeDtypeStruct((nsp, nlev, cols), s.dtype)] * 2
        out_shape += [jax.ShapeDtypeStruct((nsp, rows, cols), s.dtype)] * 2
        out_specs += [rowspec, rowspec, colspec, colspec]
    return pl.pallas_call(
        functools.partial(fix_kernel, emit),
        grid=(nsp // SB,),
        in_specs=[main, rowspec, rowspec, wrowspec, wrowspec, colspec, colspec, wcolspec, wcolspec],
        out_specs=out_specs,
        out_shape=out_shape,
        input_output_aliases={0: 0},
        cost_estimate=pl.CostEstimate(flops=8 * s.size, bytes_accessed=8 * s.size, transcendentals=0),
    )(s, ftop, fbot, wtop, wbot, fleft, fright, wleft, wright)


def advection(tracers, wind_courant):
    cols_axes = ("mp", "gy")
    rf, rl, cf, cl = edges(tracers, wind_courant)
    top, bot = exchange(rf, rl, "gx")
    left, right = exchange(cf, cl, cols_axes)
    mid = open_step(tracers, wind_courant)
    mid, srf, srl, scf, scl = fix_step(mid, top, bot, top, bot, left, right, left, right, True)
    stop, sbot = exchange(srf, srl, "gx")
    sleft, sright = exchange(scf, scl, cols_axes)
    out = open_step(mid, wind_courant)
    (out,) = fix_step(out, stop, sbot, top, bot, sleft, sright, left, right, False)
    return out


def padded_2(block, sides, width):
    (row_axes, row_dim), (col_axes, col_dim) = sides
    rows, cols = block.shape[row_dim], block.shape[col_dim]
    top, bot = exchange(lax.slice_in_dim(block, 0, 1, axis=row_dim),
                        lax.slice_in_dim(block, rows - 1, rows, axis=row_dim), row_axes)
    left, right = exchange(lax.slice_in_dim(block, 0, 1, axis=col_dim),
                           lax.slice_in_dim(block, cols - 1, cols, axis=col_dim), col_axes)
    mid = jnp.concatenate([top, block, bot], axis=row_dim)
    spec = [(0, 0)] * block.ndim
    spec[row_dim] = (1, 1)
    left = jnp.pad(left, spec)
    right = jnp.pad(right, spec)
    return jnp.concatenate([left, mid, right], axis=col_dim)


def harmonic(first_cond, second_cond):
    summed = first_cond + second_cond
    return 2.0 * first_cond * second_cond / jnp.where(summed > 0.0, summed, 1.0)


def sweep(padded, saturated, exponent, capacity, previous, surface, outside):
    conductance = saturated * jnp.exp(exponent * jnp.minimum(padded, 0.0))
    center = conductance[:, 1:-1, 1:-1]
    iterate = padded[:, 1:-1, 1:-1]
    east_face = harmonic(center, conductance[:, 2:, 1:-1])
    west_face = harmonic(center, conductance[:, :-2, 1:-1])
    north_face = harmonic(center, conductance[:, 1:-1, 2:])
    south_face = harmonic(center, conductance[:, 1:-1, :-2])
    lateral = (
        east_face * padded[:, 2:, 1:-1]
        + west_face * padded[:, :-2, 1:-1]
        + north_face * padded[:, 1:-1, 2:]
        + south_face * padded[:, 1:-1, :-2]
    )
    vertical = harmonic(center[:-1], center[1:])
    blank_layer = jnp.zeros_like(center[:1])
    below_face = jnp.concatenate([vertical, blank_layer], axis=0)
    above_face = jnp.concatenate([blank_layer, vertical], axis=0)
    inflow = jnp.concatenate([surface[None], jnp.zeros_like(center[1:])], axis=0)
    drainage = jnp.concatenate([jnp.zeros_like(center[:-1]), center[-1:]], axis=0)
    denominator = (
        capacity
        + east_face
        + west_face
        + north_face
        + south_face
        + above_face
        + below_face
        + outside
    )
    numerator = (
        capacity * previous
        + lateral
        + above_face * jnp.concatenate([blank_layer, iterate[:-1]], axis=0)
        + below_face * jnp.concatenate([iterate[1:], blank_layer], axis=0)
        + above_face
        - below_face
        + inflow
        - drainage
    )
    return numerator / denominator


def lookup(soil_kinds, values_table):
    matches = soil_kinds[None] == jnp.arange(values_table.shape[0], dtype=jnp.int32)[:, None, None]
    return jnp.sum(jnp.where(matches, values_table[:, None, None], jnp.float32(0.0)), axis=0)


def forcing_fields(advected):
    precip = jax.nn.softplus(advected[3, 0])
    evaporation = jax.nn.softplus(-advected[1, 0])
    radiation = jax.nn.sigmoid(advected[0, 0]) * jnp.exp(-jax.nn.softplus(advected[2, 0]))
    return jnp.stack([precip, evaporation, radiation], axis=0)


def on_device(
    tracers,
    wind_courant,
    pressure_head,
    storage,
    soil_type,
    land_mask,
    conductivity_table,
    exponent_table,
):
    advected = advection(tracers, wind_courant)
    received = lax.all_to_all(
        forcing_fields(advected), "gy", split_axis=1, concat_axis=2, tiled=True
    )
    surface = land_mask.astype(jnp.float32) * (received[0] - received[1] * received[2])
    saturated = lookup(soil_type, conductivity_table)
    exponent = lookup(soil_type, exponent_table)
    layers = pressure_head.shape[0]
    padded_head = padded_2(
        jnp.concatenate([pressure_head, saturated[None], exponent[None]], axis=0),
        ((("gx", "gy"), 1), ("mp", 2)),
        1,
    )
    saturated_padded = padded_head[layers]
    exponent_padded = padded_head[layers + 1]
    iterate = sweep(
        padded_head[:layers],
        saturated_padded,
        exponent_padded,
        storage,
        pressure_head,
        surface,
        0.0,
    )
    for repeat in range(SWEEPS - 1):
        padded_next = padded_2(iterate, ((("gx", "gy"), 1), ("mp", 2)), 1)
        iterate = sweep(
            padded_next, saturated_padded, exponent_padded, storage, pressure_head, surface, 0.0
        )
    return (advected, iterate)


def solution(mesh):
    placed = (
        P(None, None, "gx", ("mp", "gy")),
        P(None, None, "gx", ("mp", "gy")),
        P(None, ("gx", "gy"), "mp"),
        P(None, ("gx", "gy"), "mp"),
        P(("gx", "gy"), "mp"),
        P(("gx", "gy"), "mp"),
        P(),
        P(),
    )
    return jax.shard_map(
        on_device,
        mesh=mesh,
        in_specs=placed,
        out_specs=(P(None, None, "gx", ("mp", "gy")), P(None, ("gx", "gy"), "mp")),
        check_vma=False,
    )
```

```python
import functools
import jax
import jax.numpy as jnp
from jax import lax
from jax.experimental import pallas as pl
from jax.experimental.pallas import tpu as pltpu
from jax.sharding import PartitionSpec as P

SWEEPS = 3
SB = 2
EB = 4


def shift_pairs(count, step):
    if step > 0:
        return [(i, i + 1) for i in range(count - 1)]
    return [(i + 1, i) for i in range(count - 1)]


def edge_body(f_ref, b, rf_ref, rl_ref, cf_ref, cl_ref):
    nlev, rows, cols = f_ref.shape[1:]
    lane = lax.broadcasted_iota(jnp.int32, (rows, cols), 1)
    acc_f = jnp.zeros((rows, cols), jnp.float32)
    acc_l = jnp.zeros((rows, cols), jnp.float32)
    for lev in range(nlev):
        q = f_ref[b, lev]
        rf_ref[b, pl.ds(lev, 1), :] = q[0:1, :]
        rl_ref[b, pl.ds(lev, 1), :] = q[rows - 1:rows, :]
        at_lev = lane == lev
        acc_f = jnp.where(at_lev, pltpu.roll(q, lev, 1) if lev else q, acc_f)
        acc_l = jnp.where(at_lev, pltpu.roll(q, (lev + 1) % cols, 1), acc_l)
    cf_ref[b] = acc_f
    cl_ref[b] = acc_l


def edge_kernel(nmain, f_ref, *refs):
    if len(refs) == 5:
        w_ref, outs = refs[0], refs[1:]
    else:
        w_ref, outs = None, refs
    i = pl.program_id(0)

    @pl.when(i < nmain)
    def _():
        for b in range(f_ref.shape[0]):
            edge_body(f_ref, b, *outs)

    if w_ref is not None:
        @pl.when(i == nmain)
        def _():
            for b in range(w_ref.shape[0]):
                edge_body(w_ref, b, *outs)


def edges(f, w=None):
    n, nlev, rows, cols = f.shape
    nb = 2
    nmain = n // nb
    total = n + (0 if w is None else w.shape[0])
    row_shape = jax.ShapeDtypeStruct((total, nlev, cols), f.dtype)
    col_shape = jax.ShapeDtypeStruct((total, rows, cols), f.dtype)
    rspec = pl.BlockSpec((nb, nlev, cols), lambda i: (i, 0, 0))
    cspec = pl.BlockSpec((nb, rows, cols), lambda i: (i, 0, 0))
    in_specs = [pl.BlockSpec((nb, nlev, rows, cols), lambda i: (jnp.minimum(i, nmain - 1), 0, 0, 0))]
    args = [f]
    if w is not None:
        in_specs.append(pl.BlockSpec(w.shape, lambda i: (0, 0, 0, 0)))
        args.append(w)
    return pl.pallas_call(
        functools.partial(edge_kernel, nmain),
        grid=(total // nb,),
        in_specs=in_specs,
        out_specs=[rspec, rspec, cspec, cspec],
        out_shape=[row_shape, row_shape, col_shape, col_shape],
        cost_estimate=pl.CostEstimate(flops=4 * total * nlev * rows * cols,
                                      bytes_accessed=4 * total * nlev * rows * cols, transcendentals=0),
    )(*args)


def step_kernel(f_ref, w_ref, ftop_ref, fbot_ref, wtop_ref, wbot_ref,
                fleft_ref, fright_ref, wleft_ref, wright_ref, o_ref):
    nb, nlev, rows, cols = f_ref.shape
    row = lax.broadcasted_iota(jnp.int32, (rows, cols), 0)
    lane = lax.broadcasted_iota(jnp.int32, (rows, cols), 1)
    first_row = row == 0
    last_row = row == rows - 1
    first_lane = lane == 0
    last_lane = lane == cols - 1

    def to_first(x, lev):
        return pltpu.roll(x, (cols - lev) % cols, 1) if lev else x

    def to_last(x, lev):
        s = (cols - 1 - lev) % cols
        return pltpu.roll(x, s, 1) if s else x

    for lev in range(nlev):
        u = w_ref[0, lev]
        v = w_ref[1, lev]
        u_prev = jnp.where(first_row, wtop_ref[0, pl.ds(lev, 1), :], pltpu.roll(u, 1, 0))
        u_next = jnp.where(last_row, wbot_ref[0, pl.ds(lev, 1), :], pltpu.roll(u, rows - 1, 0))
        v_prev = jnp.where(first_lane, to_first(wleft_ref[1], lev), pltpu.roll(v, 1, 1))
        v_next = jnp.where(last_lane, to_last(wright_ref[1], lev), pltpu.roll(v, cols - 1, 1))
        pu = jnp.maximum(u, 0.0)
        mu = jnp.minimum(u, 0.0)
        pu_prev = jnp.maximum(u_prev, 0.0)
        mu_next = jnp.minimum(u_next, 0.0)
        pv = jnp.maximum(v, 0.0)
        mv = jnp.minimum(v, 0.0)
        pv_prev = jnp.maximum(v_prev, 0.0)
        mv_next = jnp.minimum(v_next, 0.0)
        for b in range(nb):
            q = f_ref[b, lev]
            q_prev = jnp.where(first_row, ftop_ref[b, pl.ds(lev, 1), :], pltpu.roll(q, 1, 0))
            q_next = jnp.where(last_row, fbot_ref[b, pl.ds(lev, 1), :], pltpu.roll(q, rows - 1, 0))
            q_w = jnp.where(first_lane, to_first(fleft_ref[b], lev), pltpu.roll(q, 1, 1))
            q_e = jnp.where(last_lane, to_last(fright_ref[b], lev), pltpu.roll(q, cols - 1, 1))
            fxp = pu * q + mu_next * q_next
            fxm = pu_prev * q_prev + mu * q
            fyp = pv * q + mv_next * q_e
            fym = pv_prev * q_w + mv * q
            o_ref[b, lev] = q - (fxp - fxm) - (fyp - fym)


def advect_step(f, w, ftop, fbot, wtop, wbot, fleft, fright, wleft, wright):
    nsp, nlev, rows, cols = f.shape
    main = pl.BlockSpec((SB, nlev, rows, cols), lambda i: (i, 0, 0, 0))
    rowspec = pl.BlockSpec((SB, nlev, cols), lambda i: (i, 0, 0))
    colspec = pl.BlockSpec((SB, rows, cols), lambda i: (i, 0, 0))
    wblock = nsp // 2
    wrowspec = pl.BlockSpec((2, nlev, cols), lambda i: (wblock, 0, 0))
    wcolspec = pl.BlockSpec((2, rows, cols), lambda i: (wblock, 0, 0))
    nbytes = 4 * (2 * f.size + w.size)
    return pl.pallas_call(
        step_kernel,
        grid=(nsp // SB,),
        in_specs=[main, pl.BlockSpec(w.shape, lambda i: (0, 0, 0, 0)), rowspec, rowspec, wrowspec, wrowspec,
                  colspec, colspec, wcolspec, wcolspec],
        out_specs=main,
        out_shape=jax.ShapeDtypeStruct(f.shape, f.dtype),
        cost_estimate=pl.CostEstimate(flops=20 * f.size, bytes_accessed=nbytes, transcendentals=0),
    )(f, w, ftop, fbot, wtop, wbot, fleft, fright, wleft, wright)


def exchange(first, last, axes):
    n = lax.axis_size(axes)
    before = lax.ppermute(last, axes, shift_pairs(n, 1))
    after = lax.ppermute(first, axes, shift_pairs(n, -1))
    return before, after


def open_kernel(f_ref, w_ref, o_ref):
    nb, nlev, rows, cols = f_ref.shape
    row = lax.broadcasted_iota(jnp.int32, (rows, cols), 0)
    lane = lax.broadcasted_iota(jnp.int32, (rows, cols), 1)
    first_row = row == 0
    last_row = row == rows - 1
    first_lane = lane == 0
    last_lane = lane == cols - 1
    for lev in range(nlev):
        u = w_ref[0, lev]
        v = w_ref[1, lev]
        u_prev = jnp.where(first_row, 0.0, pltpu.roll(u, 1, 0))
        u_next = jnp.where(last_row, 0.0, pltpu.roll(u, rows - 1, 0))
        v_prev = jnp.where(first_lane, 0.0, pltpu.roll(v, 1, 1))
        v_next = jnp.where(last_lane, 0.0, pltpu.roll(v, cols - 1, 1))
        pu = jnp.maximum(u, 0.0)
        mu = jnp.minimum(u, 0.0)
        pu_prev = jnp.maximum(u_prev, 0.0)
        mu_next = jnp.minimum(u_next, 0.0)
        pv = jnp.maximum(v, 0.0)
        mv = jnp.minimum(v, 0.0)
        pv_prev = jnp.maximum(v_prev, 0.0)
        mv_next = jnp.minimum(v_next, 0.0)
        for b in range(nb):
            q = f_ref[b, lev]
            q_prev = pltpu.roll(q, 1, 0)
            q_next = pltpu.roll(q, rows - 1, 0)
            q_w = pltpu.roll(q, 1, 1)
            q_e = pltpu.roll(q, cols - 1, 1)
            fxp = pu * q + mu_next * q_next
            fxm = pu_prev * q_prev + mu * q
            fyp = pv * q + mv_next * q_e
            fym = pv_prev * q_w + mv * q
            o_ref[b, lev] = q - (fxp - fxm) - (fyp - fym)


def open_step(f, w):
    nsp, nlev, rows, cols = f.shape
    main = pl.BlockSpec((SB, nlev, rows, cols), lambda i: (i, 0, 0, 0))
    return pl.pallas_call(
        open_kernel,
        grid=(nsp // SB,),
        in_specs=[main, pl.BlockSpec(w.shape, lambda i: (0, 0, 0, 0))],
        out_specs=main,
        out_shape=jax.ShapeDtypeStruct(f.shape, f.dtype),
        cost_estimate=pl.CostEstimate(flops=20 * f.size, bytes_accessed=4 * (2 * f.size + w.size),
                                      transcendentals=0),
    )(f, w)


def fix_kernel(emit, s_ref, ftop_ref, fbot_ref, wtop_ref, wbot_ref, fleft_ref, fright_ref,
               wleft_ref, wright_ref, o_ref, *edge_refs):
    nb, nlev, rows, cols = s_ref.shape
    row = lax.broadcasted_iota(jnp.int32, (rows, cols), 0)
    lane = lax.broadcasted_iota(jnp.int32, (rows, cols), 1)
    first_row = row == 0
    last_row = row == rows - 1
    first_lane = lane == 0
    last_lane = lane == cols - 1

    def to_first(x, lev):
        return pltpu.roll(x, (cols - lev) % cols, 1) if lev else x

    def to_last(x, lev):
        sh = (cols - 1 - lev) % cols
        return pltpu.roll(x, sh, 1) if sh else x

    if emit:
        rf_ref, rl_ref, cf_ref, cl_ref = edge_refs
    wl = wleft_ref[1]
    wr = wright_ref[1]
    for b in range(nb):
        acc_f = jnp.zeros((rows, cols), jnp.float32)
        acc_l = jnp.zeros((rows, cols), jnp.float32)
        fl = fleft_ref[b]
        fr = fright_ref[b]
        for lev in range(nlev):
            x = s_ref[b, lev]
            top = jnp.maximum(wtop_ref[0, pl.ds(lev, 1), :], 0.0) * ftop_ref[b, pl.ds(lev, 1), :]
            bot = jnp.minimum(wbot_ref[0, pl.ds(lev, 1), :], 0.0) * fbot_ref[b, pl.ds(lev, 1), :]
            left = jnp.maximum(to_first(wl, lev), 0.0) * to_first(fl, lev)
            right = jnp.minimum(to_last(wr, lev), 0.0) * to_last(fr, lev)
            x = jnp.where(first_row, x + top, x)
            x = jnp.where(last_row, x - bot, x)
            x = jnp.where(first_lane, x + left, x)
            x = jnp.where(last_lane, x - right, x)
            o_ref[b, lev] = x
            if emit:
                rf_ref[b, pl.ds(lev, 1), :] = x[0:1, :]
                rl_ref[b, pl.ds(lev, 1), :] = x[rows - 1:rows, :]
                at_lev = lane == lev
                acc_f = jnp.where(at_lev, pltpu.roll(x, lev, 1) if lev else x, acc_f)
                acc_l = jnp.where(at_lev, pltpu.roll(x, (lev + 1) % cols, 1), acc_l)
        if emit:
            cf_ref[b] = acc_f
            cl_ref[b] = acc_l


def fix_step(s, ftop, fbot, wtop, wbot, fleft, fright, wleft, wright, emit):
    nsp, nlev, rows, cols = s.shape
    main = pl.BlockSpec((SB, nlev, rows, cols), lambda i: (i, 0, 0, 0))
    rowspec = pl.BlockSpec((SB, nlev, cols), lambda i: (i, 0, 0))
    colspec = pl.BlockSpec((SB, rows, cols), lambda i: (i, 0, 0))
    wrowspec = pl.BlockSpec((2, nlev, cols), lambda i: (wtop.shape[0] // 2 - 1, 0, 0))
    wcolspec = pl.BlockSpec((2, rows, cols), lambda i: (wleft.shape[0] // 2 - 1, 0, 0))
    out_shape = [jax.ShapeDtypeStruct(s.shape, s.dtype)]
    out_specs = [main]
    if emit:
        out_shape += [jax.ShapeDtypeStruct((nsp, nlev, cols), s.dtype)] * 2
        out_shape += [jax.ShapeDtypeStruct((nsp, rows, cols), s.dtype)] * 2
        out_specs += [rowspec, rowspec, colspec, colspec]
    return pl.pallas_call(
        functools.partial(fix_kernel, emit),
        grid=(nsp // SB,),
        in_specs=[main, rowspec, rowspec, wrowspec, wrowspec, colspec, colspec, wcolspec, wcolspec],
        out_specs=out_specs,
        out_shape=out_shape,
        input_output_aliases={0: 0},
        cost_estimate=pl.CostEstimate(flops=8 * s.size, bytes_accessed=8 * s.size, transcendentals=0),
    )(s, ftop, fbot, wtop, wbot, fleft, fright, wleft, wright)


def advection(tracers, wind_courant):
    cols_axes = ("mp", "gy")
    rf, rl, cf, cl = edges(tracers, wind_courant)
    top, bot = exchange(rf, rl, "gx")
    left, right = exchange(cf, cl, cols_axes)
    mid = open_step(tracers, wind_courant)
    (mid,) = fix_step(mid, top, bot, top, bot, left, right, left, right, False)
    srf, srl, scf, scl = edges(mid)
    stop, sbot = exchange(srf, srl, "gx")
    sleft, sright = exchange(scf, scl, cols_axes)
    out = open_step(mid, wind_courant)
    (out,) = fix_step(out, stop, sbot, top, bot, sleft, sright, left, right, False)
    return out


def padded_2(block, sides, width):
    (row_axes, row_dim), (col_axes, col_dim) = sides
    rows, cols = block.shape[row_dim], block.shape[col_dim]
    top, bot = exchange(lax.slice_in_dim(block, 0, 1, axis=row_dim),
                        lax.slice_in_dim(block, rows - 1, rows, axis=row_dim), row_axes)
    left, right = exchange(lax.slice_in_dim(block, 0, 1, axis=col_dim),
                           lax.slice_in_dim(block, cols - 1, cols, axis=col_dim), col_axes)
    mid = jnp.concatenate([top, block, bot], axis=row_dim)
    spec = [(0, 0)] * block.ndim
    spec[row_dim] = (1, 1)
    left = jnp.pad(left, spec)
    right = jnp.pad(right, spec)
    return jnp.concatenate([left, mid, right], axis=col_dim)


def harmonic(first_cond, second_cond):
    summed = first_cond + second_cond
    return 2.0 * first_cond * second_cond / jnp.where(summed > 0.0, summed, 1.0)


def sweep(padded, saturated, exponent, capacity, previous, surface, outside):
    conductance = saturated * jnp.exp(exponent * jnp.minimum(padded, 0.0))
    center = conductance[:, 1:-1, 1:-1]
    iterate = padded[:, 1:-1, 1:-1]
    east_face = harmonic(center, conductance[:, 2:, 1:-1])
    west_face = harmonic(center, conductance[:, :-2, 1:-1])
    north_face = harmonic(center, conductance[:, 1:-1, 2:])
    south_face = harmonic(center, conductance[:, 1:-1, :-2])
    lateral = (
        east_face * padded[:, 2:, 1:-1]
        + west_face * padded[:, :-2, 1:-1]
        + north_face * padded[:, 1:-1, 2:]
        + south_face * padded[:, 1:-1, :-2]
    )
    vertical = harmonic(center[:-1], center[1:])
    blank_layer = jnp.zeros_like(center[:1])
    below_face = jnp.concatenate([vertical, blank_layer], axis=0)
    above_face = jnp.concatenate([blank_layer, vertical], axis=0)
    inflow = jnp.concatenate([surface[None], jnp.zeros_like(center[1:])], axis=0)
    drainage = jnp.concatenate([jnp.zeros_like(center[:-1]), center[-1:]], axis=0)
    denominator = (
        capacity
        + east_face
        + west_face
        + north_face
        + south_face
        + above_face
        + below_face
        + outside
    )
    numerator = (
        capacity * previous
        + lateral
        + above_face * jnp.concatenate([blank_layer, iterate[:-1]], axis=0)
        + below_face * jnp.concatenate([iterate[1:], blank_layer], axis=0)
        + above_face
        - below_face
        + inflow
        - drainage
    )
    return numerator / denominator


def lookup(soil_kinds, values_table):
    matches = soil_kinds[None] == jnp.arange(values_table.shape[0], dtype=jnp.int32)[:, None, None]
    return jnp.sum(jnp.where(matches, values_table[:, None, None], jnp.float32(0.0)), axis=0)


def forcing_fields(advected):
    precip = jax.nn.softplus(advected[3, 0])
    evaporation = jax.nn.softplus(-advected[1, 0])
    radiation = jax.nn.sigmoid(advected[0, 0]) * jnp.exp(-jax.nn.softplus(advected[2, 0]))
    return jnp.stack([precip, evaporation, radiation], axis=0)


def on_device(
    tracers,
    wind_courant,
    pressure_head,
    storage,
    soil_type,
    land_mask,
    conductivity_table,
    exponent_table,
):
    advected = advection(tracers, wind_courant)
    received = lax.all_to_all(
        forcing_fields(advected), "gy", split_axis=1, concat_axis=2, tiled=True
    )
    surface = land_mask.astype(jnp.float32) * (received[0] - received[1] * received[2])
    saturated = lookup(soil_type, conductivity_table)
    exponent = lookup(soil_type, exponent_table)
    layers = pressure_head.shape[0]
    padded_head = padded_2(
        jnp.concatenate([pressure_head, saturated[None], exponent[None]], axis=0),
        ((("gx", "gy"), 1), ("mp", 2)),
        1,
    )
    saturated_padded = padded_head[layers]
    exponent_padded = padded_head[layers + 1]
    iterate = sweep(
        padded_head[:layers],
        saturated_padded,
        exponent_padded,
        storage,
        pressure_head,
        surface,
        0.0,
    )
    for repeat in range(SWEEPS - 1):
        padded_next = padded_2(iterate, ((("gx", "gy"), 1), ("mp", 2)), 1)
        iterate = sweep(
            padded_next, saturated_padded, exponent_padded, storage, pressure_head, surface, 0.0
        )
    return (advected, iterate)


def solution(mesh):
    placed = (
        P(None, None, "gx", ("mp", "gy")),
        P(None, None, "gx", ("mp", "gy")),
        P(None, ("gx", "gy"), "mp"),
        P(None, ("gx", "gy"), "mp"),
        P(("gx", "gy"), "mp"),
        P(("gx", "gy"), "mp"),
        P(),
        P(),
    )
    return jax.shard_map(
        on_device,
        mesh=mesh,
        in_specs=placed,
        out_specs=(P(None, None, "gx", ("mp", "gy")), P(None, ("gx", "gy"), "mp")),
        check_vma=False,
    )
```

```python
import functools
import jax
import jax.numpy as jnp
from jax import lax
from jax.experimental import pallas as pl
from jax.experimental.pallas import tpu as pltpu
from jax.sharding import PartitionSpec as P

SWEEPS = 3
SB = 2
EB = 4


def shift_pairs(count, step):
    if step > 0:
        return [(i, i + 1) for i in range(count - 1)]
    return [(i + 1, i) for i in range(count - 1)]


def edge_body(f_ref, b, rf_ref, rl_ref, cf_ref, cl_ref):
    nlev, rows, cols = f_ref.shape[1:]
    lane = lax.broadcasted_iota(jnp.int32, (rows, cols), 1)
    acc_f = jnp.zeros((rows, cols), jnp.float32)
    acc_l = jnp.zeros((rows, cols), jnp.float32)
    for lev in range(nlev):
        q = f_ref[b, lev]
        rf_ref[b, pl.ds(lev, 1), :] = q[0:1, :]
        rl_ref[b, pl.ds(lev, 1), :] = q[rows - 1:rows, :]
        at_lev = lane == lev
        acc_f = jnp.where(at_lev, pltpu.roll(q, lev, 1) if lev else q, acc_f)
        acc_l = jnp.where(at_lev, pltpu.roll(q, (lev + 1) % cols, 1), acc_l)
    cf_ref[b] = acc_f
    cl_ref[b] = acc_l


def edge_kernel(nmain, f_ref, *refs):
    if len(refs) == 5:
        w_ref, outs = refs[0], refs[1:]
    else:
        w_ref, outs = None, refs
    i = pl.program_id(0)

    @pl.when(i < nmain)
    def _():
        for b in range(f_ref.shape[0]):
            edge_body(f_ref, b, *outs)

    if w_ref is not None:
        @pl.when(i == nmain)
        def _():
            for b in range(w_ref.shape[0]):
                edge_body(w_ref, b, *outs)


def edges(f, w=None):
    n, nlev, rows, cols = f.shape
    nb = 2
    nmain = n // nb
    total = n + (0 if w is None else w.shape[0])
    row_shape = jax.ShapeDtypeStruct((total, nlev, cols), f.dtype)
    col_shape = jax.ShapeDtypeStruct((total, rows, cols), f.dtype)
    rspec = pl.BlockSpec((nb, nlev, cols), lambda i: (i, 0, 0))
    cspec = pl.BlockSpec((nb, rows, cols), lambda i: (i, 0, 0))
    in_specs = [pl.BlockSpec((nb, nlev, rows, cols), lambda i: (jnp.minimum(i, nmain - 1), 0, 0, 0))]
    args = [f]
    if w is not None:
        in_specs.append(pl.BlockSpec(w.shape, lambda i: (0, 0, 0, 0)))
        args.append(w)
    return pl.pallas_call(
        functools.partial(edge_kernel, nmain),
        grid=(total // nb,),
        in_specs=in_specs,
        out_specs=[rspec, rspec, cspec, cspec],
        out_shape=[row_shape, row_shape, col_shape, col_shape],
        cost_estimate=pl.CostEstimate(flops=4 * total * nlev * rows * cols,
                                      bytes_accessed=4 * total * nlev * rows * cols, transcendentals=0),
    )(*args)


def step_kernel(emit, f_ref, w_ref, ftop_ref, fbot_ref, wtop_ref, wbot_ref,
                fleft_ref, fright_ref, wleft_ref, wright_ref, o_ref, *edge_refs):
    nb, nlev, rows, cols = f_ref.shape
    row = lax.broadcasted_iota(jnp.int32, (rows, cols), 0)
    lane = lax.broadcasted_iota(jnp.int32, (rows, cols), 1)
    sub = lax.broadcasted_iota(jnp.int32, (8, cols), 0)
    first_row = row == 0
    last_row = row == rows - 1
    first_lane = lane == 0
    last_lane = lane == cols - 1

    def to_first(x, lev):
        return pltpu.roll(x, (cols - lev) % cols, 1) if lev else x

    def to_last(x, lev):
        sh = (cols - 1 - lev) % cols
        return pltpu.roll(x, sh, 1) if sh else x

    zero_tile = jnp.zeros((8, cols), jnp.float32)
    zero_plane = jnp.zeros((rows, cols), jnp.float32)
    acc_rf = [zero_tile] * nb
    acc_rl = [zero_tile] * nb
    acc_cf = [zero_plane] * nb
    acc_cl = [zero_plane] * nb
    for lev in range(nlev):
        u = w_ref[0, lev]
        v = w_ref[1, lev]
        u_prev = jnp.where(first_row, wtop_ref[0, pl.ds(lev, 1), :], pltpu.roll(u, 1, 0))
        u_next = jnp.where(last_row, wbot_ref[0, pl.ds(lev, 1), :], pltpu.roll(u, rows - 1, 0))
        v_prev = jnp.where(first_lane, to_first(wleft_ref[1], lev), pltpu.roll(v, 1, 1))
        v_next = jnp.where(last_lane, to_last(wright_ref[1], lev), pltpu.roll(v, cols - 1, 1))
        pu = jnp.maximum(u, 0.0)
        mu = jnp.minimum(u, 0.0)
        pu_prev = jnp.maximum(u_prev, 0.0)
        mu_next = jnp.minimum(u_next, 0.0)
        pv = jnp.maximum(v, 0.0)
        mv = jnp.minimum(v, 0.0)
        pv_prev = jnp.maximum(v_prev, 0.0)
        mv_next = jnp.minimum(v_next, 0.0)
        at_lev = lane == lev
        at_sub = sub == lev % 8
        for b in range(nb):
            q = f_ref[b, lev]
            q_prev = jnp.where(first_row, ftop_ref[b, pl.ds(lev, 1), :], pltpu.roll(q, 1, 0))
            q_next = jnp.where(last_row, fbot_ref[b, pl.ds(lev, 1), :], pltpu.roll(q, rows - 1, 0))
            q_w = jnp.where(first_lane, to_first(fleft_ref[b], lev), pltpu.roll(q, 1, 1))
            q_e = jnp.where(last_lane, to_last(fright_ref[b], lev), pltpu.roll(q, cols - 1, 1))
            fxp = pu * q + mu_next * q_next
            fxm = pu_prev * q_prev + mu * q
            fyp = pv * q + mv_next * q_e
            fym = pv_prev * q_w + mv * q
            new = q - (fxp - fxm) - (fyp - fym)
            o_ref[b, lev] = new
            if emit:
                acc_rf[b] = jnp.where(at_sub, new[0:1, :], acc_rf[b])
                acc_rl[b] = jnp.where(at_sub, new[rows - 1:rows, :], acc_rl[b])
                acc_cf[b] = jnp.where(at_lev, pltpu.roll(new, lev, 1) if lev else new, acc_cf[b])
                acc_cl[b] = jnp.where(at_lev, pltpu.roll(new, (lev + 1) % cols, 1), acc_cl[b])
        if emit and (lev % 8 == 7 or lev == nlev - 1):
            rf_ref, rl_ref = edge_refs[0], edge_refs[1]
            base = (lev // 8) * 8
            for b in range(nb):
                rf_ref[b, base:base + 8, :] = acc_rf[b]
                rl_ref[b, base:base + 8, :] = acc_rl[b]
    if emit:
        cf_ref, cl_ref = edge_refs[2], edge_refs[3]
        for b in range(nb):
            cf_ref[b] = acc_cf[b]
            cl_ref[b] = acc_cl[b]


def advect_step(f, w, ftop, fbot, wtop, wbot, fleft, fright, wleft, wright, emit=False):
    nsp, nlev, rows, cols = f.shape
    main = pl.BlockSpec((SB, nlev, rows, cols), lambda i: (i, 0, 0, 0))
    rowspec = pl.BlockSpec((SB, ftop.shape[1], cols), lambda i: (i, 0, 0))
    colspec = pl.BlockSpec((SB, rows, cols), lambda i: (i, 0, 0))
    wblock = nsp // 2
    wrowspec = pl.BlockSpec((2, wtop.shape[1], cols), lambda i: (wblock, 0, 0))
    wcolspec = pl.BlockSpec((2, rows, cols), lambda i: (wblock, 0, 0))
    nbytes = 4 * (2 * f.size + w.size)
    out_shape = [jax.ShapeDtypeStruct(f.shape, f.dtype)]
    out_specs = [main]
    if emit:
        padded_lev = ((nlev + 7) // 8) * 8
        out_shape += [jax.ShapeDtypeStruct((nsp, padded_lev, cols), f.dtype)] * 2
        out_shape += [jax.ShapeDtypeStruct((nsp, rows, cols), f.dtype)] * 2
        out_specs += [pl.BlockSpec((SB, padded_lev, cols), lambda i: (i, 0, 0))] * 2 + [colspec] * 2
    return pl.pallas_call(
        functools.partial(step_kernel, emit),
        grid=(nsp // SB,),
        in_specs=[main, pl.BlockSpec(w.shape, lambda i: (0, 0, 0, 0)), rowspec, rowspec, wrowspec, wrowspec,
                  colspec, colspec, wcolspec, wcolspec],
        out_specs=out_specs,
        out_shape=out_shape,
        cost_estimate=pl.CostEstimate(flops=20 * f.size, bytes_accessed=nbytes, transcendentals=0),
    )(f, w, ftop, fbot, wtop, wbot, fleft, fright, wleft, wright)


def exchange(first, last, axes):
    n = lax.axis_size(axes)
    before = lax.ppermute(last, axes, shift_pairs(n, 1))
    after = lax.ppermute(first, axes, shift_pairs(n, -1))
    return before, after


def advection(tracers, wind_courant):
    cols_axes = ("mp", "gy")
    rf, rl, cf, cl = edges(tracers, wind_courant)
    top, bot = exchange(rf, rl, "gx")
    left, right = exchange(cf, cl, cols_axes)
    mid, srf, srl, scf, scl = advect_step(tracers, wind_courant, top, bot, top, bot, left, right, left, right,
                                          emit=True)
    stop, sbot = exchange(srf, srl, "gx")
    sleft, sright = exchange(scf, scl, cols_axes)
    return advect_step(mid, wind_courant, stop, sbot, top, bot, sleft, sright, left, right)[0]


def padded_2(block, sides, width):
    (row_axes, row_dim), (col_axes, col_dim) = sides
    rows, cols = block.shape[row_dim], block.shape[col_dim]
    top, bot = exchange(lax.slice_in_dim(block, 0, 1, axis=row_dim),
                        lax.slice_in_dim(block, rows - 1, rows, axis=row_dim), row_axes)
    left, right = exchange(lax.slice_in_dim(block, 0, 1, axis=col_dim),
                           lax.slice_in_dim(block, cols - 1, cols, axis=col_dim), col_axes)
    mid = jnp.concatenate([top, block, bot], axis=row_dim)
    spec = [(0, 0)] * block.ndim
    spec[row_dim] = (1, 1)
    left = jnp.pad(left, spec)
    right = jnp.pad(right, spec)
    return jnp.concatenate([left, mid, right], axis=col_dim)


def harmonic(first_cond, second_cond):
    summed = first_cond + second_cond
    return 2.0 * first_cond * second_cond / jnp.where(summed > 0.0, summed, 1.0)


def sweep(padded, saturated, exponent, capacity, previous, surface, outside):
    conductance = saturated * jnp.exp(exponent * jnp.minimum(padded, 0.0))
    center = conductance[:, 1:-1, 1:-1]
    iterate = padded[:, 1:-1, 1:-1]
    east_face = harmonic(center, conductance[:, 2:, 1:-1])
    west_face = harmonic(center, conductance[:, :-2, 1:-1])
    north_face = harmonic(center, conductance[:, 1:-1, 2:])
    south_face = harmonic(center, conductance[:, 1:-1, :-2])
    lateral = (
        east_face * padded[:, 2:, 1:-1]
        + west_face * padded[:, :-2, 1:-1]
        + north_face * padded[:, 1:-1, 2:]
        + south_face * padded[:, 1:-1, :-2]
    )
    vertical = harmonic(center[:-1], center[1:])
    blank_layer = jnp.zeros_like(center[:1])
    below_face = jnp.concatenate([vertical, blank_layer], axis=0)
    above_face = jnp.concatenate([blank_layer, vertical], axis=0)
    inflow = jnp.concatenate([surface[None], jnp.zeros_like(center[1:])], axis=0)
    drainage = jnp.concatenate([jnp.zeros_like(center[:-1]), center[-1:]], axis=0)
    denominator = (
        capacity
        + east_face
        + west_face
        + north_face
        + south_face
        + above_face
        + below_face
        + outside
    )
    numerator = (
        capacity * previous
        + lateral
        + above_face * jnp.concatenate([blank_layer, iterate[:-1]], axis=0)
        + below_face * jnp.concatenate([iterate[1:], blank_layer], axis=0)
        + above_face
        - below_face
        + inflow
        - drainage
    )
    return numerator / denominator


def lookup(soil_kinds, values_table):
    matches = soil_kinds[None] == jnp.arange(values_table.shape[0], dtype=jnp.int32)[:, None, None]
    return jnp.sum(jnp.where(matches, values_table[:, None, None], jnp.float32(0.0)), axis=0)


def forcing_fields(advected):
    precip = jax.nn.softplus(advected[3, 0])
    evaporation = jax.nn.softplus(-advected[1, 0])
    radiation = jax.nn.sigmoid(advected[0, 0]) * jnp.exp(-jax.nn.softplus(advected[2, 0]))
    return jnp.stack([precip, evaporation, radiation], axis=0)


def on_device(
    tracers,
    wind_courant,
    pressure_head,
    storage,
    soil_type,
    land_mask,
    conductivity_table,
    exponent_table,
):
    advected = advection(tracers, wind_courant)
    received = lax.all_to_all(
        forcing_fields(advected), "gy", split_axis=1, concat_axis=2, tiled=True
    )
    surface = land_mask.astype(jnp.float32) * (received[0] - received[1] * received[2])
    saturated = lookup(soil_type, conductivity_table)
    exponent = lookup(soil_type, exponent_table)
    layers = pressure_head.shape[0]
    padded_head = padded_2(
        jnp.concatenate([pressure_head, saturated[None], exponent[None]], axis=0),
        ((("gx", "gy"), 1), ("mp", 2)),
        1,
    )
    saturated_padded = padded_head[layers]
    exponent_padded = padded_head[layers + 1]
    iterate = sweep(
        padded_head[:layers],
        saturated_padded,
        exponent_padded,
        storage,
        pressure_head,
        surface,
        0.0,
    )
    for repeat in range(SWEEPS - 1):
        padded_next = padded_2(iterate, ((("gx", "gy"), 1), ("mp", 2)), 1)
        iterate = sweep(
            padded_next, saturated_padded, exponent_padded, storage, pressure_head, surface, 0.0
        )
    return (advected, iterate)


def solution(mesh):
    placed = (
        P(None, None, "gx", ("mp", "gy")),
        P(None, None, "gx", ("mp", "gy")),
        P(None, ("gx", "gy"), "mp"),
        P(None, ("gx", "gy"), "mp"),
        P(("gx", "gy"), "mp"),
        P(("gx", "gy"), "mp"),
        P(),
        P(),
    )
    return jax.shard_map(
        on_device,
        mesh=mesh,
        in_specs=placed,
        out_specs=(P(None, None, "gx", ("mp", "gy")), P(None, ("gx", "gy"), "mp")),
        check_vma=False,
    )
```

```python
import functools
import jax
import jax.numpy as jnp
from jax import lax
from jax.experimental import pallas as pl
from jax.experimental.pallas import tpu as pltpu
from jax.sharding import PartitionSpec as P

SWEEPS = 3
SB = 4
EB = 4


def shift_pairs(count, step):
    if step > 0:
        return [(i, i + 1) for i in range(count - 1)]
    return [(i + 1, i) for i in range(count - 1)]


def edge_body(f_ref, b, rf_ref, rl_ref, cf_ref, cl_ref):
    nlev, rows, cols = f_ref.shape[1:]
    lane = lax.broadcasted_iota(jnp.int32, (rows, cols), 1)
    acc_f = jnp.zeros((rows, cols), jnp.float32)
    acc_l = jnp.zeros((rows, cols), jnp.float32)
    for lev in range(nlev):
        q = f_ref[b, lev]
        rf_ref[b, pl.ds(lev, 1), :] = q[0:1, :]
        rl_ref[b, pl.ds(lev, 1), :] = q[rows - 1:rows, :]
        at_lev = lane == lev
        acc_f = jnp.where(at_lev, pltpu.roll(q, lev, 1) if lev else q, acc_f)
        acc_l = jnp.where(at_lev, pltpu.roll(q, (lev + 1) % cols, 1), acc_l)
    cf_ref[b] = acc_f
    cl_ref[b] = acc_l


def edge_kernel(nmain, f_ref, *refs):
    if len(refs) == 5:
        w_ref, outs = refs[0], refs[1:]
    else:
        w_ref, outs = None, refs
    i = pl.program_id(0)

    @pl.when(i < nmain)
    def _():
        for b in range(f_ref.shape[0]):
            edge_body(f_ref, b, *outs)

    if w_ref is not None:
        @pl.when(i == nmain)
        def _():
            for b in range(w_ref.shape[0]):
                edge_body(w_ref, b, *outs)


def edges(f, w=None):
    n, nlev, rows, cols = f.shape
    nb = 2
    nmain = n // nb
    total = n + (0 if w is None else w.shape[0])
    row_shape = jax.ShapeDtypeStruct((total, nlev, cols), f.dtype)
    col_shape = jax.ShapeDtypeStruct((total, rows, cols), f.dtype)
    rspec = pl.BlockSpec((nb, nlev, cols), lambda i: (i, 0, 0))
    cspec = pl.BlockSpec((nb, rows, cols), lambda i: (i, 0, 0))
    in_specs = [pl.BlockSpec((nb, nlev, rows, cols), lambda i: (jnp.minimum(i, nmain - 1), 0, 0, 0))]
    args = [f]
    if w is not None:
        in_specs.append(pl.BlockSpec(w.shape, lambda i: (0, 0, 0, 0)))
        args.append(w)
    return pl.pallas_call(
        functools.partial(edge_kernel, nmain),
        grid=(total // nb,),
        in_specs=in_specs,
        out_specs=[rspec, rspec, cspec, cspec],
        out_shape=[row_shape, row_shape, col_shape, col_shape],
        cost_estimate=pl.CostEstimate(flops=4 * total * nlev * rows * cols,
                                      bytes_accessed=4 * total * nlev * rows * cols, transcendentals=0),
    )(*args)


def step_kernel(f_ref, w_ref, ftop_ref, fbot_ref, wtop_ref, wbot_ref,
                fleft_ref, fright_ref, wleft_ref, wright_ref, o_ref):
    nb, nlev, rows, cols = f_ref.shape
    row = lax.broadcasted_iota(jnp.int32, (rows, cols), 0)
    lane = lax.broadcasted_iota(jnp.int32, (rows, cols), 1)
    first_row = row == 0
    last_row = row == rows - 1
    first_lane = lane == 0
    last_lane = lane == cols - 1

    def to_first(x, lev):
        return pltpu.roll(x, (cols - lev) % cols, 1) if lev else x

    def to_last(x, lev):
        s = (cols - 1 - lev) % cols
        return pltpu.roll(x, s, 1) if s else x

    for lev in range(nlev):
        u = w_ref[0, lev]
        v = w_ref[1, lev]
        u_prev = jnp.where(first_row, wtop_ref[0, pl.ds(lev, 1), :], pltpu.roll(u, 1, 0))
        u_next = jnp.where(last_row, wbot_ref[0, pl.ds(lev, 1), :], pltpu.roll(u, rows - 1, 0))
        v_prev = jnp.where(first_lane, to_first(wleft_ref[1], lev), pltpu.roll(v, 1, 1))
        v_next = jnp.where(last_lane, to_last(wright_ref[1], lev), pltpu.roll(v, cols - 1, 1))
        pu = jnp.maximum(u, 0.0)
        mu = jnp.minimum(u, 0.0)
        pu_prev = jnp.maximum(u_prev, 0.0)
        mu_next = jnp.minimum(u_next, 0.0)
        pv = jnp.maximum(v, 0.0)
        mv = jnp.minimum(v, 0.0)
        pv_prev = jnp.maximum(v_prev, 0.0)
        mv_next = jnp.minimum(v_next, 0.0)
        for b in range(nb):
            q = f_ref[b, lev]
            q_prev = jnp.where(first_row, ftop_ref[b, pl.ds(lev, 1), :], pltpu.roll(q, 1, 0))
            q_next = jnp.where(last_row, fbot_ref[b, pl.ds(lev, 1), :], pltpu.roll(q, rows - 1, 0))
            q_w = jnp.where(first_lane, to_first(fleft_ref[b], lev), pltpu.roll(q, 1, 1))
            q_e = jnp.where(last_lane, to_last(fright_ref[b], lev), pltpu.roll(q, cols - 1, 1))
            fxp = pu * q + mu_next * q_next
            fxm = pu_prev * q_prev + mu * q
            fyp = pv * q + mv_next * q_e
            fym = pv_prev * q_w + mv * q
            o_ref[b, lev] = q - (fxp - fxm) - (fyp - fym)


def advect_step(f, w, ftop, fbot, wtop, wbot, fleft, fright, wleft, wright):
    nsp, nlev, rows, cols = f.shape
    main = pl.BlockSpec((SB, nlev, rows, cols), lambda i: (i, 0, 0, 0))
    rowspec = pl.BlockSpec((SB, nlev, cols), lambda i: (i, 0, 0))
    colspec = pl.BlockSpec((SB, rows, cols), lambda i: (i, 0, 0))
    wblock = nsp // 2
    wrowspec = pl.BlockSpec((2, nlev, cols), lambda i: (wblock, 0, 0))
    wcolspec = pl.BlockSpec((2, rows, cols), lambda i: (wblock, 0, 0))
    nbytes = 4 * (2 * f.size + w.size)
    return pl.pallas_call(
        step_kernel,
        grid=(nsp // SB,),
        in_specs=[main, pl.BlockSpec(w.shape, lambda i: (0, 0, 0, 0)), rowspec, rowspec, wrowspec, wrowspec,
                  colspec, colspec, wcolspec, wcolspec],
        out_specs=main,
        out_shape=jax.ShapeDtypeStruct(f.shape, f.dtype),
        cost_estimate=pl.CostEstimate(flops=20 * f.size, bytes_accessed=nbytes, transcendentals=0),
    )(f, w, ftop, fbot, wtop, wbot, fleft, fright, wleft, wright)


def exchange(first, last, axes):
    n = lax.axis_size(axes)
    before = lax.ppermute(last, axes, shift_pairs(n, 1))
    after = lax.ppermute(first, axes, shift_pairs(n, -1))
    return before, after


def advection(tracers, wind_courant):
    cols_axes = ("mp", "gy")
    rf, rl, cf, cl = edges(tracers, wind_courant)
    top, bot = exchange(rf, rl, "gx")
    left, right = exchange(cf, cl, cols_axes)
    mid = advect_step(tracers, wind_courant, top, bot, top, bot, left, right, left, right)
    srf, srl, scf, scl = edges(mid)
    stop, sbot = exchange(srf, srl, "gx")
    sleft, sright = exchange(scf, scl, cols_axes)
    return advect_step(mid, wind_courant, stop, sbot, top, bot, sleft, sright, left, right)


def padded_2(block, sides, width):
    (row_axes, row_dim), (col_axes, col_dim) = sides
    rows, cols = block.shape[row_dim], block.shape[col_dim]
    top, bot = exchange(lax.slice_in_dim(block, 0, 1, axis=row_dim),
                        lax.slice_in_dim(block, rows - 1, rows, axis=row_dim), row_axes)
    left, right = exchange(lax.slice_in_dim(block, 0, 1, axis=col_dim),
                           lax.slice_in_dim(block, cols - 1, cols, axis=col_dim), col_axes)
    mid = jnp.concatenate([top, block, bot], axis=row_dim)
    spec = [(0, 0)] * block.ndim
    spec[row_dim] = (1, 1)
    left = jnp.pad(left, spec)
    right = jnp.pad(right, spec)
    return jnp.concatenate([left, mid, right], axis=col_dim)


def harmonic(first_cond, second_cond):
    summed = first_cond + second_cond
    return 2.0 * first_cond * second_cond / jnp.where(summed > 0.0, summed, 1.0)


def sweep(padded, saturated, exponent, capacity, previous, surface, outside):
    conductance = saturated * jnp.exp(exponent * jnp.minimum(padded, 0.0))
    center = conductance[:, 1:-1, 1:-1]
    iterate = padded[:, 1:-1, 1:-1]
    east_face = harmonic(center, conductance[:, 2:, 1:-1])
    west_face = harmonic(center, conductance[:, :-2, 1:-1])
    north_face = harmonic(center, conductance[:, 1:-1, 2:])
    south_face = harmonic(center, conductance[:, 1:-1, :-2])
    lateral = (
        east_face * padded[:, 2:, 1:-1]
        + west_face * padded[:, :-2, 1:-1]
        + north_face * padded[:, 1:-1, 2:]
        + south_face * padded[:, 1:-1, :-2]
    )
    vertical = harmonic(center[:-1], center[1:])
    blank_layer = jnp.zeros_like(center[:1])
    below_face = jnp.concatenate([vertical, blank_layer], axis=0)
    above_face = jnp.concatenate([blank_layer, vertical], axis=0)
    inflow = jnp.concatenate([surface[None], jnp.zeros_like(center[1:])], axis=0)
    drainage = jnp.concatenate([jnp.zeros_like(center[:-1]), center[-1:]], axis=0)
    denominator = (
        capacity
        + east_face
        + west_face
        + north_face
        + south_face
        + above_face
        + below_face
        + outside
    )
    numerator = (
        capacity * previous
        + lateral
        + above_face * jnp.concatenate([blank_layer, iterate[:-1]], axis=0)
        + below_face * jnp.concatenate([iterate[1:], blank_layer], axis=0)
        + above_face
        - below_face
        + inflow
        - drainage
    )
    return numerator / denominator


def lookup(soil_kinds, values_table):
    matches = soil_kinds[None] == jnp.arange(values_table.shape[0], dtype=jnp.int32)[:, None, None]
    return jnp.sum(jnp.where(matches, values_table[:, None, None], jnp.float32(0.0)), axis=0)


def forcing_fields(advected):
    precip = jax.nn.softplus(advected[3, 0])
    evaporation = jax.nn.softplus(-advected[1, 0])
    radiation = jax.nn.sigmoid(advected[0, 0]) * jnp.exp(-jax.nn.softplus(advected[2, 0]))
    return jnp.stack([precip, evaporation, radiation], axis=0)


def on_device(
    tracers,
    wind_courant,
    pressure_head,
    storage,
    soil_type,
    land_mask,
    conductivity_table,
    exponent_table,
):
    advected = advection(tracers, wind_courant)
    received = lax.all_to_all(
        forcing_fields(advected), "gy", split_axis=1, concat_axis=2, tiled=True
    )
    surface = land_mask.astype(jnp.float32) * (received[0] - received[1] * received[2])
    saturated = lookup(soil_type, conductivity_table)
    exponent = lookup(soil_type, exponent_table)
    layers = pressure_head.shape[0]
    padded_head = padded_2(
        jnp.concatenate([pressure_head, saturated[None], exponent[None]], axis=0),
        ((("gx", "gy"), 1), ("mp", 2)),
        1,
    )
    saturated_padded = padded_head[layers]
    exponent_padded = padded_head[layers + 1]
    iterate = sweep(
        padded_head[:layers],
        saturated_padded,
        exponent_padded,
        storage,
        pressure_head,
        surface,
        0.0,
    )
    for repeat in range(SWEEPS - 1):
        padded_next = padded_2(iterate, ((("gx", "gy"), 1), ("mp", 2)), 1)
        iterate = sweep(
            padded_next, saturated_padded, exponent_padded, storage, pressure_head, surface, 0.0
        )
    return (advected, iterate)


def solution(mesh):
    placed = (
        P(None, None, "gx", ("mp", "gy")),
        P(None, None, "gx", ("mp", "gy")),
        P(None, ("gx", "gy"), "mp"),
        P(None, ("gx", "gy"), "mp"),
        P(("gx", "gy"), "mp"),
        P(("gx", "gy"), "mp"),
        P(),
        P(),
    )
    return jax.shard_map(
        on_device,
        mesh=mesh,
        in_specs=placed,
        out_specs=(P(None, None, "gx", ("mp", "gy")), P(None, ("gx", "gy"), "mp")),
        check_vma=False,
    )
```

```python
import functools
import jax
import jax.numpy as jnp
from jax import lax
from jax.experimental import pallas as pl
from jax.experimental.pallas import tpu as pltpu
from jax.sharding import PartitionSpec as P

SWEEPS = 3
SB = 4
EB = 4


def shift_pairs(count, step):
    if step > 0:
        return [(i, i + 1) for i in range(count - 1)]
    return [(i + 1, i) for i in range(count - 1)]


def edge_body(f_ref, b, rf_ref, rl_ref, cf_ref, cl_ref):
    nlev, rows, cols = f_ref.shape[1:]
    lane = lax.broadcasted_iota(jnp.int32, (rows, cols), 1)
    acc_f = jnp.zeros((rows, cols), jnp.float32)
    acc_l = jnp.zeros((rows, cols), jnp.float32)
    for lev in range(nlev):
        q = f_ref[b, lev]
        rf_ref[b, pl.ds(lev, 1), :] = q[0:1, :]
        rl_ref[b, pl.ds(lev, 1), :] = q[rows - 1:rows, :]
        at_lev = lane == lev
        acc_f = jnp.where(at_lev, pltpu.roll(q, lev, 1) if lev else q, acc_f)
        acc_l = jnp.where(at_lev, pltpu.roll(q, (lev + 1) % cols, 1), acc_l)
    cf_ref[b] = acc_f
    cl_ref[b] = acc_l


def edge_kernel(nmain, f_ref, *refs):
    if len(refs) == 5:
        w_ref, outs = refs[0], refs[1:]
    else:
        w_ref, outs = None, refs
    i = pl.program_id(0)

    @pl.when(i < nmain)
    def _():
        for b in range(f_ref.shape[0]):
            edge_body(f_ref, b, *outs)

    if w_ref is not None:
        @pl.when(i == nmain)
        def _():
            for b in range(w_ref.shape[0]):
                edge_body(w_ref, b, *outs)
            for b in range(w_ref.shape[0], outs[0].shape[0]):
                for out in outs:
                    out[b] = jnp.zeros(out.shape[1:], out.dtype)


def edges(f, w=None):
    n, nlev, rows, cols = f.shape
    nb = 4
    nmain = n // nb
    total = n + (0 if w is None else nb)
    row_shape = jax.ShapeDtypeStruct((total, nlev, cols), f.dtype)
    col_shape = jax.ShapeDtypeStruct((total, rows, cols), f.dtype)
    rspec = pl.BlockSpec((nb, nlev, cols), lambda i: (i, 0, 0))
    cspec = pl.BlockSpec((nb, rows, cols), lambda i: (i, 0, 0))
    in_specs = [pl.BlockSpec((nb, nlev, rows, cols), lambda i: (jnp.minimum(i, nmain - 1), 0, 0, 0))]
    args = [f]
    if w is not None:
        in_specs.append(pl.BlockSpec(w.shape, lambda i: (0, 0, 0, 0)))
        args.append(w)
    return pl.pallas_call(
        functools.partial(edge_kernel, nmain),
        grid=(total // nb,),
        in_specs=in_specs,
        out_specs=[rspec, rspec, cspec, cspec],
        out_shape=[row_shape, row_shape, col_shape, col_shape],
        cost_estimate=pl.CostEstimate(flops=4 * total * nlev * rows * cols,
                                      bytes_accessed=4 * total * nlev * rows * cols, transcendentals=0),
    )(*args)


def step_kernel(f_ref, w_ref, ftop_ref, fbot_ref, wtop_ref, wbot_ref,
                fleft_ref, fright_ref, wleft_ref, wright_ref, o_ref):
    nb, nlev, rows, cols = f_ref.shape
    row = lax.broadcasted_iota(jnp.int32, (rows, cols), 0)
    lane = lax.broadcasted_iota(jnp.int32, (rows, cols), 1)
    first_row = row == 0
    last_row = row == rows - 1
    first_lane = lane == 0
    last_lane = lane == cols - 1

    def to_first(x, lev):
        return pltpu.roll(x, (cols - lev) % cols, 1) if lev else x

    def to_last(x, lev):
        s = (cols - 1 - lev) % cols
        return pltpu.roll(x, s, 1) if s else x

    for lev in range(nlev):
        u = w_ref[0, lev]
        v = w_ref[1, lev]
        u_prev = jnp.where(first_row, wtop_ref[0, pl.ds(lev, 1), :], pltpu.roll(u, 1, 0))
        u_next = jnp.where(last_row, wbot_ref[0, pl.ds(lev, 1), :], pltpu.roll(u, rows - 1, 0))
        v_prev = jnp.where(first_lane, to_first(wleft_ref[1], lev), pltpu.roll(v, 1, 1))
        v_next = jnp.where(last_lane, to_last(wright_ref[1], lev), pltpu.roll(v, cols - 1, 1))
        pu = jnp.maximum(u, 0.0)
        mu = jnp.minimum(u, 0.0)
        pu_prev = jnp.maximum(u_prev, 0.0)
        mu_next = jnp.minimum(u_next, 0.0)
        pv = jnp.maximum(v, 0.0)
        mv = jnp.minimum(v, 0.0)
        pv_prev = jnp.maximum(v_prev, 0.0)
        mv_next = jnp.minimum(v_next, 0.0)
        for b in range(nb):
            q = f_ref[b, lev]
            q_prev = jnp.where(first_row, ftop_ref[b, pl.ds(lev, 1), :], pltpu.roll(q, 1, 0))
            q_next = jnp.where(last_row, fbot_ref[b, pl.ds(lev, 1), :], pltpu.roll(q, rows - 1, 0))
            q_w = jnp.where(first_lane, to_first(fleft_ref[b], lev), pltpu.roll(q, 1, 1))
            q_e = jnp.where(last_lane, to_last(fright_ref[b], lev), pltpu.roll(q, cols - 1, 1))
            fxp = pu * q + mu_next * q_next
            fxm = pu_prev * q_prev + mu * q
            fyp = pv * q + mv_next * q_e
            fym = pv_prev * q_w + mv * q
            o_ref[b, lev] = q - (fxp - fxm) - (fyp - fym)


def advect_step(f, w, ftop, fbot, wtop, wbot, fleft, fright, wleft, wright):
    nsp, nlev, rows, cols = f.shape
    main = pl.BlockSpec((SB, nlev, rows, cols), lambda i: (i, 0, 0, 0))
    rowspec = pl.BlockSpec((SB, nlev, cols), lambda i: (i, 0, 0))
    colspec = pl.BlockSpec((SB, rows, cols), lambda i: (i, 0, 0))
    wblock = nsp // 2
    wrowspec = pl.BlockSpec((2, nlev, cols), lambda i: (wblock, 0, 0))
    wcolspec = pl.BlockSpec((2, rows, cols), lambda i: (wblock, 0, 0))
    nbytes = 4 * (2 * f.size + w.size)
    return pl.pallas_call(
        step_kernel,
        grid=(nsp // SB,),
        in_specs=[main, pl.BlockSpec(w.shape, lambda i: (0, 0, 0, 0)), rowspec, rowspec, wrowspec, wrowspec,
                  colspec, colspec, wcolspec, wcolspec],
        out_specs=main,
        out_shape=jax.ShapeDtypeStruct(f.shape, f.dtype),
        cost_estimate=pl.CostEstimate(flops=20 * f.size, bytes_accessed=nbytes, transcendentals=0),
    )(f, w, ftop, fbot, wtop, wbot, fleft, fright, wleft, wright)


def exchange(first, last, axes):
    n = lax.axis_size(axes)
    before = lax.ppermute(last, axes, shift_pairs(n, 1))
    after = lax.ppermute(first, axes, shift_pairs(n, -1))
    return before, after


def advection(tracers, wind_courant):
    cols_axes = ("mp", "gy")
    rf, rl, cf, cl = edges(tracers, wind_courant)
    top, bot = exchange(rf, rl, "gx")
    left, right = exchange(cf, cl, cols_axes)
    mid = advect_step(tracers, wind_courant, top, bot, top, bot, left, right, left, right)
    srf, srl, scf, scl = edges(mid)
    stop, sbot = exchange(srf, srl, "gx")
    sleft, sright = exchange(scf, scl, cols_axes)
    return advect_step(mid, wind_courant, stop, sbot, top, bot, sleft, sright, left, right)


def padded_2(block, sides, width):
    (row_axes, row_dim), (col_axes, col_dim) = sides
    rows, cols = block.shape[row_dim], block.shape[col_dim]
    top, bot = exchange(lax.slice_in_dim(block, 0, 1, axis=row_dim),
                        lax.slice_in_dim(block, rows - 1, rows, axis=row_dim), row_axes)
    left, right = exchange(lax.slice_in_dim(block, 0, 1, axis=col_dim),
                           lax.slice_in_dim(block, cols - 1, cols, axis=col_dim), col_axes)
    mid = jnp.concatenate([top, block, bot], axis=row_dim)
    spec = [(0, 0)] * block.ndim
    spec[row_dim] = (1, 1)
    left = jnp.pad(left, spec)
    right = jnp.pad(right, spec)
    return jnp.concatenate([left, mid, right], axis=col_dim)


def harmonic(first_cond, second_cond):
    summed = first_cond + second_cond
    return 2.0 * first_cond * second_cond / jnp.where(summed > 0.0, summed, 1.0)


def sweep(padded, saturated, exponent, capacity, previous, surface, outside):
    conductance = saturated * jnp.exp(exponent * jnp.minimum(padded, 0.0))
    center = conductance[:, 1:-1, 1:-1]
    iterate = padded[:, 1:-1, 1:-1]
    east_face = harmonic(center, conductance[:, 2:, 1:-1])
    west_face = harmonic(center, conductance[:, :-2, 1:-1])
    north_face = harmonic(center, conductance[:, 1:-1, 2:])
    south_face = harmonic(center, conductance[:, 1:-1, :-2])
    lateral = (
        east_face * padded[:, 2:, 1:-1]
        + west_face * padded[:, :-2, 1:-1]
        + north_face * padded[:, 1:-1, 2:]
        + south_face * padded[:, 1:-1, :-2]
    )
    vertical = harmonic(center[:-1], center[1:])
    blank_layer = jnp.zeros_like(center[:1])
    below_face = jnp.concatenate([vertical, blank_layer], axis=0)
    above_face = jnp.concatenate([blank_layer, vertical], axis=0)
    inflow = jnp.concatenate([surface[None], jnp.zeros_like(center[1:])], axis=0)
    drainage = jnp.concatenate([jnp.zeros_like(center[:-1]), center[-1:]], axis=0)
    denominator = (
        capacity
        + east_face
        + west_face
        + north_face
        + south_face
        + above_face
        + below_face
        + outside
    )
    numerator = (
        capacity * previous
        + lateral
        + above_face * jnp.concatenate([blank_layer, iterate[:-1]], axis=0)
        + below_face * jnp.concatenate([iterate[1:], blank_layer], axis=0)
        + above_face
        - below_face
        + inflow
        - drainage
    )
    return numerator / denominator


def lookup(soil_kinds, values_table):
    matches = soil_kinds[None] == jnp.arange(values_table.shape[0], dtype=jnp.int32)[:, None, None]
    return jnp.sum(jnp.where(matches, values_table[:, None, None], jnp.float32(0.0)), axis=0)


def forcing_fields(advected):
    precip = jax.nn.softplus(advected[3, 0])
    evaporation = jax.nn.softplus(-advected[1, 0])
    radiation = jax.nn.sigmoid(advected[0, 0]) * jnp.exp(-jax.nn.softplus(advected[2, 0]))
    return jnp.stack([precip, evaporation, radiation], axis=0)


def on_device(
    tracers,
    wind_courant,
    pressure_head,
    storage,
    soil_type,
    land_mask,
    conductivity_table,
    exponent_table,
):
    advected = advection(tracers, wind_courant)
    received = lax.all_to_all(
        forcing_fields(advected), "gy", split_axis=1, concat_axis=2, tiled=True
    )
    surface = land_mask.astype(jnp.float32) * (received[0] - received[1] * received[2])
    saturated = lookup(soil_type, conductivity_table)
    exponent = lookup(soil_type, exponent_table)
    layers = pressure_head.shape[0]
    padded_head = padded_2(
        jnp.concatenate([pressure_head, saturated[None], exponent[None]], axis=0),
        ((("gx", "gy"), 1), ("mp", 2)),
        1,
    )
    saturated_padded = padded_head[layers]
    exponent_padded = padded_head[layers + 1]
    iterate = sweep(
        padded_head[:layers],
        saturated_padded,
        exponent_padded,
        storage,
        pressure_head,
        surface,
        0.0,
    )
    for repeat in range(SWEEPS - 1):
        padded_next = padded_2(iterate, ((("gx", "gy"), 1), ("mp", 2)), 1)
        iterate = sweep(
            padded_next, saturated_padded, exponent_padded, storage, pressure_head, surface, 0.0
        )
    return (advected, iterate)


def solution(mesh):
    placed = (
        P(None, None, "gx", ("mp", "gy")),
        P(None, None, "gx", ("mp", "gy")),
        P(None, ("gx", "gy"), "mp"),
        P(None, ("gx", "gy"), "mp"),
        P(("gx", "gy"), "mp"),
        P(("gx", "gy"), "mp"),
        P(),
        P(),
    )
    return jax.shard_map(
        on_device,
        mesh=mesh,
        in_specs=placed,
        out_specs=(P(None, None, "gx", ("mp", "gy")), P(None, ("gx", "gy"), "mp")),
        check_vma=False,
    )
```

```python
import functools
import jax
import jax.numpy as jnp
from jax import lax
from jax.experimental import pallas as pl
from jax.experimental.pallas import tpu as pltpu
from jax.sharding import PartitionSpec as P

SWEEPS = 3
SB = 8
EB = 4


def shift_pairs(count, step):
    if step > 0:
        return [(i, i + 1) for i in range(count - 1)]
    return [(i + 1, i) for i in range(count - 1)]


def edge_body(f_ref, b, rf_ref, rl_ref, cf_ref, cl_ref):
    nlev, rows, cols = f_ref.shape[1:]
    lane = lax.broadcasted_iota(jnp.int32, (rows, cols), 1)
    acc_f = jnp.zeros((rows, cols), jnp.float32)
    acc_l = jnp.zeros((rows, cols), jnp.float32)
    for lev in range(nlev):
        q = f_ref[b, lev]
        rf_ref[b, pl.ds(lev, 1), :] = q[0:1, :]
        rl_ref[b, pl.ds(lev, 1), :] = q[rows - 1:rows, :]
        at_lev = lane == lev
        acc_f = jnp.where(at_lev, pltpu.roll(q, lev, 1) if lev else q, acc_f)
        acc_l = jnp.where(at_lev, pltpu.roll(q, (lev + 1) % cols, 1), acc_l)
    cf_ref[b] = acc_f
    cl_ref[b] = acc_l


def edge_kernel(nmain, f_ref, *refs):
    if len(refs) == 5:
        w_ref, outs = refs[0], refs[1:]
    else:
        w_ref, outs = None, refs
    i = pl.program_id(0)

    @pl.when(i < nmain)
    def _():
        for b in range(f_ref.shape[0]):
            edge_body(f_ref, b, *outs)

    if w_ref is not None:
        @pl.when(i == nmain)
        def _():
            for b in range(w_ref.shape[0]):
                edge_body(w_ref, b, *outs)
            for b in range(w_ref.shape[0], outs[0].shape[0]):
                for out in outs:
                    out[b] = jnp.zeros(out.shape[1:], out.dtype)


def edges(f, w=None):
    n, nlev, rows, cols = f.shape
    nb = 4
    nmain = n // nb
    total = n + (0 if w is None else nb)
    row_shape = jax.ShapeDtypeStruct((total, nlev, cols), f.dtype)
    col_shape = jax.ShapeDtypeStruct((total, rows, cols), f.dtype)
    rspec = pl.BlockSpec((nb, nlev, cols), lambda i: (i, 0, 0))
    cspec = pl.BlockSpec((nb, rows, cols), lambda i: (i, 0, 0))
    in_specs = [pl.BlockSpec((nb, nlev, rows, cols), lambda i: (jnp.minimum(i, nmain - 1), 0, 0, 0))]
    args = [f]
    if w is not None:
        in_specs.append(pl.BlockSpec(w.shape, lambda i: (0, 0, 0, 0)))
        args.append(w)
    return pl.pallas_call(
        functools.partial(edge_kernel, nmain),
        grid=(total // nb,),
        in_specs=in_specs,
        out_specs=[rspec, rspec, cspec, cspec],
        out_shape=[row_shape, row_shape, col_shape, col_shape],
        cost_estimate=pl.CostEstimate(flops=4 * total * nlev * rows * cols,
                                      bytes_accessed=4 * total * nlev * rows * cols, transcendentals=0),
    )(*args)


def step_kernel(f_ref, w_ref, ftop_ref, fbot_ref, wtop_ref, wbot_ref,
                fleft_ref, fright_ref, wleft_ref, wright_ref, o_ref):
    nb, nlev, rows, cols = f_ref.shape
    row = lax.broadcasted_iota(jnp.int32, (rows, cols), 0)
    lane = lax.broadcasted_iota(jnp.int32, (rows, cols), 1)
    first_row = row == 0
    last_row = row == rows - 1
    first_lane = lane == 0
    last_lane = lane == cols - 1

    def to_first(x, lev):
        return pltpu.roll(x, (cols - lev) % cols, 1) if lev else x

    def to_last(x, lev):
        s = (cols - 1 - lev) % cols
        return pltpu.roll(x, s, 1) if s else x

    for lev in range(nlev):
        u = w_ref[0, lev]
        v = w_ref[1, lev]
        u_prev = jnp.where(first_row, wtop_ref[0, pl.ds(lev, 1), :], pltpu.roll(u, 1, 0))
        u_next = jnp.where(last_row, wbot_ref[0, pl.ds(lev, 1), :], pltpu.roll(u, rows - 1, 0))
        v_prev = jnp.where(first_lane, to_first(wleft_ref[1], lev), pltpu.roll(v, 1, 1))
        v_next = jnp.where(last_lane, to_last(wright_ref[1], lev), pltpu.roll(v, cols - 1, 1))
        pu = jnp.maximum(u, 0.0)
        mu = jnp.minimum(u, 0.0)
        pu_prev = jnp.maximum(u_prev, 0.0)
        mu_next = jnp.minimum(u_next, 0.0)
        pv = jnp.maximum(v, 0.0)
        mv = jnp.minimum(v, 0.0)
        pv_prev = jnp.maximum(v_prev, 0.0)
        mv_next = jnp.minimum(v_next, 0.0)
        for b in range(nb):
            q = f_ref[b, lev]
            q_prev = jnp.where(first_row, ftop_ref[b, pl.ds(lev, 1), :], pltpu.roll(q, 1, 0))
            q_next = jnp.where(last_row, fbot_ref[b, pl.ds(lev, 1), :], pltpu.roll(q, rows - 1, 0))
            q_w = jnp.where(first_lane, to_first(fleft_ref[b], lev), pltpu.roll(q, 1, 1))
            q_e = jnp.where(last_lane, to_last(fright_ref[b], lev), pltpu.roll(q, cols - 1, 1))
            fxp = pu * q + mu_next * q_next
            fxm = pu_prev * q_prev + mu * q
            fyp = pv * q + mv_next * q_e
            fym = pv_prev * q_w + mv * q
            o_ref[b, lev] = q - (fxp - fxm) - (fyp - fym)


def advect_step(f, w, ftop, fbot, wtop, wbot, fleft, fright, wleft, wright):
    nsp, nlev, rows, cols = f.shape
    main = pl.BlockSpec((SB, nlev, rows, cols), lambda i: (i, 0, 0, 0))
    rowspec = pl.BlockSpec((SB, nlev, cols), lambda i: (i, 0, 0))
    colspec = pl.BlockSpec((SB, rows, cols), lambda i: (i, 0, 0))
    wblock = nsp // 2
    wrowspec = pl.BlockSpec((2, nlev, cols), lambda i: (wblock, 0, 0))
    wcolspec = pl.BlockSpec((2, rows, cols), lambda i: (wblock, 0, 0))
    nbytes = 4 * (2 * f.size + w.size)
    return pl.pallas_call(
        step_kernel,
        grid=(nsp // SB,),
        in_specs=[main, pl.BlockSpec(w.shape, lambda i: (0, 0, 0, 0)), rowspec, rowspec, wrowspec, wrowspec,
                  colspec, colspec, wcolspec, wcolspec],
        out_specs=main,
        out_shape=jax.ShapeDtypeStruct(f.shape, f.dtype),
        cost_estimate=pl.CostEstimate(flops=20 * f.size, bytes_accessed=nbytes, transcendentals=0),
    )(f, w, ftop, fbot, wtop, wbot, fleft, fright, wleft, wright)


def exchange(first, last, axes):
    n = lax.axis_size(axes)
    before = lax.ppermute(last, axes, shift_pairs(n, 1))
    after = lax.ppermute(first, axes, shift_pairs(n, -1))
    return before, after


def advection(tracers, wind_courant):
    cols_axes = ("mp", "gy")
    rf, rl, cf, cl = edges(tracers, wind_courant)
    top, bot = exchange(rf, rl, "gx")
    left, right = exchange(cf, cl, cols_axes)
    mid = advect_step(tracers, wind_courant, top, bot, top, bot, left, right, left, right)
    srf, srl, scf, scl = edges(mid)
    stop, sbot = exchange(srf, srl, "gx")
    sleft, sright = exchange(scf, scl, cols_axes)
    return advect_step(mid, wind_courant, stop, sbot, top, bot, sleft, sright, left, right)


def padded_2(block, sides, width):
    (row_axes, row_dim), (col_axes, col_dim) = sides
    rows, cols = block.shape[row_dim], block.shape[col_dim]
    top, bot = exchange(lax.slice_in_dim(block, 0, 1, axis=row_dim),
                        lax.slice_in_dim(block, rows - 1, rows, axis=row_dim), row_axes)
    left, right = exchange(lax.slice_in_dim(block, 0, 1, axis=col_dim),
                           lax.slice_in_dim(block, cols - 1, cols, axis=col_dim), col_axes)
    mid = jnp.concatenate([top, block, bot], axis=row_dim)
    spec = [(0, 0)] * block.ndim
    spec[row_dim] = (1, 1)
    left = jnp.pad(left, spec)
    right = jnp.pad(right, spec)
    return jnp.concatenate([left, mid, right], axis=col_dim)


def harmonic(first_cond, second_cond):
    summed = first_cond + second_cond
    return 2.0 * first_cond * second_cond / jnp.where(summed > 0.0, summed, 1.0)


def sweep(padded, saturated, exponent, capacity, previous, surface, outside):
    conductance = saturated * jnp.exp(exponent * jnp.minimum(padded, 0.0))
    center = conductance[:, 1:-1, 1:-1]
    iterate = padded[:, 1:-1, 1:-1]
    east_face = harmonic(center, conductance[:, 2:, 1:-1])
    west_face = harmonic(center, conductance[:, :-2, 1:-1])
    north_face = harmonic(center, conductance[:, 1:-1, 2:])
    south_face = harmonic(center, conductance[:, 1:-1, :-2])
    lateral = (
        east_face * padded[:, 2:, 1:-1]
        + west_face * padded[:, :-2, 1:-1]
        + north_face * padded[:, 1:-1, 2:]
        + south_face * padded[:, 1:-1, :-2]
    )
    vertical = harmonic(center[:-1], center[1:])
    blank_layer = jnp.zeros_like(center[:1])
    below_face = jnp.concatenate([vertical, blank_layer], axis=0)
    above_face = jnp.concatenate([blank_layer, vertical], axis=0)
    inflow = jnp.concatenate([surface[None], jnp.zeros_like(center[1:])], axis=0)
    drainage = jnp.concatenate([jnp.zeros_like(center[:-1]), center[-1:]], axis=0)
    denominator = (
        capacity
        + east_face
        + west_face
        + north_face
        + south_face
        + above_face
        + below_face
        + outside
    )
    numerator = (
        capacity * previous
        + lateral
        + above_face * jnp.concatenate([blank_layer, iterate[:-1]], axis=0)
        + below_face * jnp.concatenate([iterate[1:], blank_layer], axis=0)
        + above_face
        - below_face
        + inflow
        - drainage
    )
    return numerator / denominator


def lookup(soil_kinds, values_table):
    matches = soil_kinds[None] == jnp.arange(values_table.shape[0], dtype=jnp.int32)[:, None, None]
    return jnp.sum(jnp.where(matches, values_table[:, None, None], jnp.float32(0.0)), axis=0)


def forcing_fields(advected):
    precip = jax.nn.softplus(advected[3, 0])
    evaporation = jax.nn.softplus(-advected[1, 0])
    radiation = jax.nn.sigmoid(advected[0, 0]) * jnp.exp(-jax.nn.softplus(advected[2, 0]))
    return jnp.stack([precip, evaporation, radiation], axis=0)


def on_device(
    tracers,
    wind_courant,
    pressure_head,
    storage,
    soil_type,
    land_mask,
    conductivity_table,
    exponent_table,
):
    advected = advection(tracers, wind_courant)
    received = lax.all_to_all(
        forcing_fields(advected), "gy", split_axis=1, concat_axis=2, tiled=True
    )
    surface = land_mask.astype(jnp.float32) * (received[0] - received[1] * received[2])
    saturated = lookup(soil_type, conductivity_table)
    exponent = lookup(soil_type, exponent_table)
    layers = pressure_head.shape[0]
    padded_head = padded_2(
        jnp.concatenate([pressure_head, saturated[None], exponent[None]], axis=0),
        ((("gx", "gy"), 1), ("mp", 2)),
        1,
    )
    saturated_padded = padded_head[layers]
    exponent_padded = padded_head[layers + 1]
    iterate = sweep(
        padded_head[:layers],
        saturated_padded,
        exponent_padded,
        storage,
        pressure_head,
        surface,
        0.0,
    )
    for repeat in range(SWEEPS - 1):
        padded_next = padded_2(iterate, ((("gx", "gy"), 1), ("mp", 2)), 1)
        iterate = sweep(
            padded_next, saturated_padded, exponent_padded, storage, pressure_head, surface, 0.0
        )
    return (advected, iterate)


def solution(mesh):
    placed = (
        P(None, None, "gx", ("mp", "gy")),
        P(None, None, "gx", ("mp", "gy")),
        P(None, ("gx", "gy"), "mp"),
        P(None, ("gx", "gy"), "mp"),
        P(("gx", "gy"), "mp"),
        P(("gx", "gy"), "mp"),
        P(),
        P(),
    )
    return jax.shard_map(
        on_device,
        mesh=mesh,
        in_specs=placed,
        out_specs=(P(None, None, "gx", ("mp", "gy")), P(None, ("gx", "gy"), "mp")),
        check_vma=False,
    )
```
